128 devices in a mesh: seg: 16 (over x_hi, z, core), chan: 8 (over y, x_lo).
Axes of the slice: x: 4 (x_hi: 2, x_lo: 2; x = x_hi * 2 + x_lo), y: 4, z: 4, core: 2. Of those that a mesh axis runs over, the one named last changes fastest.
Arguments:
- signal: bfloat16 [4096, 32768], P('chan', 'seg'), may hold values from -64 to 64
- spatial: float32 [4096, 64], P('chan'), may hold values from -0.09375 to 0.09375
- temporal: float32 [64, 256], replicated, may hold values from -5 to 5
- start_codes: float32 [64, 32768], P(None, 'seg'), may hold values from -1.2 to 1.2
- thresholds: float32 [64], replicated, may hold values from 0.05 to 0.3
- step_sizes: float32 [64], replicated, may hold values from 0.03 to 0.1
- breaks: int32 [16], replicated, may hold values from 0 to 32767, as said below
Outputs:
- final_codes: float32 [64, 32768], P(None, 'seg')
- space_atoms: float32 [4096, 64], P('chan')
- time_atoms: float32 [64, 256], replicated
The draws below stay inside these ranges and needn't reach their ends.
Inputs may be any that keep to these rules, and one draw needn't show every extreme that they name: `breaks`: Increasing; one break lies in each of the 16 equal stretches of the window.
All inputs are finite; a program needn't handle non-finite values.
Results may differ from the reference program's by a relative error of at most 0.0058.
Values may be sent and summed in bfloat16 or wider, within the bound.
No kernel may reach another device: no remote copies, remote signals or barrier semaphores. Data moves between devices by JAX's collectives and lax.ppermute only.
A program may use at most 128 MiB of HBM per device.

```python
import math
import jax
import jax.numpy as jnp
from jax import lax

C = 4096
K = 64
L = 256
ITERS = 10
OUTER = 2
NB = 16
TIME = 32768


def draw_signal(key, part):
    chan_key, time_key, noise_key = jax.random.split(key, 3)
    rising = jnp.exp(jnp.log(3.0) * jnp.arange(C, dtype=jnp.float32) / C)
    chan_scale = rising * jnp.exp(jax.random.uniform(chan_key, (C,), jnp.float32, -0.6931, 0.6931))
    time_scale = jnp.exp(jax.random.uniform(time_key, (TIME,), jnp.float32, -0.6931, 0.6931))
    noise_field = jnp.clip(jax.random.normal(noise_key, (C, TIME), jnp.float32), -4.0, 4.0)
    return (chan_scale[:, None] * time_scale[None, :] * noise_field).astype(jnp.bfloat16)


def draw_breaks(key, part):
    stretch = TIME // NB
    offsets = jax.random.randint(key, (NB,), 0, stretch, dtype=jnp.int32)
    return (jnp.arange(NB, dtype=jnp.int32) * stretch + offsets).astype(jnp.int32)


def level_of(own_key, dims, cuts, smallest, largest):
    level, own = 1.0, jax.random.fold_in(own_key, 6)
    for dim, parts in cuts:
        steps = jnp.exp(jax.random.uniform(jax.random.fold_in(own, dim), (parts,), jnp.float32, smallest / len(cuts), largest / len(cuts)))
        level = level * jnp.repeat(steps, dims[dim] // parts).reshape([-1 if axis == dim else 1 for axis in range(len(dims))])
    return level


def normal_values(stream_key, shape, width, reach, shards=(), held_as=jnp.bfloat16):
    drawn = jax.random.normal(stream_key, shape, jnp.float32) * width
    if len(shards) > 0:
        drawn = level_of(stream_key, shape, shards, -0.22, 0.18) * drawn
    return jnp.clip(drawn, min=-reach, max=reach).astype(held_as)


def setup_inputs(seed: int = 0) -> dict:
    streams_of = jax.random.split(jax.random.key(seed), 8)
    signal = draw_signal(jax.random.fold_in(streams_of[7], 71), 0)
    spatial = normal_values(streams_of[1], (C, K), C ** -0.5, 0.09375, ((0, 8),), jnp.float32)
    temporal = normal_values(streams_of[2], (K, L), 1.0, 5.0, (), jnp.float32)
    start_codes = normal_values(streams_of[3], (K, TIME), 0.3, 1.2, ((1, 16),), jnp.float32)
    thresholds = jnp.clip(jnp.exp(jax.random.uniform(streams_of[4], (K,), jnp.float32, math.log(0.05), math.log(0.3))), 0.05, 0.3)
    step_sizes = jnp.clip(jnp.exp(jax.random.uniform(streams_of[5], (K,), jnp.float32, math.log(0.03), math.log(0.1))), 0.03, 0.1)
    breaks = draw_breaks(jax.random.fold_in(streams_of[7], 71), 0)
    return dict(signal=signal, spatial=spatial, temporal=temporal, start_codes=start_codes, thresholds=thresholds, step_sizes=step_sizes, breaks=breaks)


epsilon = 1e-06
highest = lax.Precision.HIGHEST

def rounded(values):
    return lax.optimization_barrier(values.astype(jnp.bfloat16)).astype(jnp.float32)

def unit_columns(matrix):
    return matrix / jnp.sqrt(lax.optimization_barrier(jnp.sum(matrix * matrix, axis=0, keepdims=True)) + epsilon)

def unit_rows(matrix):
    return matrix / jnp.sqrt(lax.optimization_barrier(jnp.sum(matrix * matrix, axis=1, keepdims=True)) + epsilon)

def spectrum(values):
    return jnp.fft.rfft(values, n=2 * TIME, axis=-1)

def convolve(kernel, latent):
    return jnp.fft.irfft(spectrum(kernel) * spectrum(latent), n=2 * TIME, axis=-1)[:, :TIME]

def correlate(kernel, residual):
    return jnp.fft.irfft(jnp.conj(spectrum(kernel)) * spectrum(residual), n=2 * TIME, axis=-1)[:, :TIME]

def lag_stats(residual, latent):
    return jnp.fft.irfft(spectrum(residual) * jnp.conj(spectrum(latent)), n=2 * TIME, axis=-1)[:, :L]

def reference(signal, spatial, temporal, start_codes, thresholds, step_sizes, breaks):
    positions = jnp.arange(TIME, dtype=jnp.int32)
    crosses = (positions[None, :] < breaks[:, None]) & (breaks[:, None] < positions[None, :] + L)
    allowed = jnp.where(jnp.any(crosses, axis=0), 0.0, 1.0).astype(jnp.float32)
    space_atoms = unit_columns(spatial)
    kernel = unit_rows(temporal)
    gram_matrix = jnp.dot(space_atoms.T, space_atoms, precision=highest)
    latent = start_codes
    step_col = step_sizes[:, None]
    limit_col = (step_sizes * thresholds)[:, None]
    for sweep_index in range(OUTER):
        projected = jnp.dot(space_atoms.astype(jnp.bfloat16).T, signal, preferred_element_type=jnp.float32)
        kernel_r = rounded(kernel)
        for iteration in range(ITERS):
            rebuilt = convolve(kernel_r, rounded(latent))
            residual = projected - jnp.dot(gram_matrix, rebuilt, precision=highest)
            descent = correlate(kernel_r, rounded(residual))
            stepped = latent + step_col * descent
            latent = allowed[None, :] * jnp.sign(stepped) * jnp.maximum(jnp.abs(stepped) - limit_col, 0.0)
        latent_r = rounded(latent)
        rebuilt = convolve(kernel_r, latent_r)
        row_stats = jnp.dot(signal, rebuilt.astype(jnp.bfloat16).T, preferred_element_type=jnp.float32)
        cross_gram = jnp.dot(rebuilt, rebuilt.T, precision=highest)
        raw_space = row_stats - jnp.dot(space_atoms, cross_gram - jnp.diag(jnp.diag(cross_gram)), precision=highest)
        others = projected - jnp.dot(gram_matrix - jnp.diag(jnp.diag(gram_matrix)), rebuilt, precision=highest)
        raw_kernel = lag_stats(others, latent_r)
        space_atoms = unit_columns(raw_space)
        kernel = unit_rows(raw_kernel)
        gram_matrix = jnp.dot(space_atoms.T, space_atoms, precision=highest)
    return (latent, space_atoms, kernel)
```

```python
import jax
import jax.numpy as jnp
from jax import lax
from jax.sharding import PartitionSpec as P

ITERS = 10
OUTER = 2


epsilon = 1e-06
highest = lax.Precision.HIGHEST


def passed_along(value, axis, steps):
    count = lax.axis_size(axis)
    leading, last = (max(0, -steps), min(count, count - steps))
    return lax.ppermute(value, axis, [(source, source + steps) for source in range(leading, last)])


def butterfly_sum(value, axis):
    count = lax.axis_size(axis)
    distance = 1
    while distance < count:
        partner = lax.ppermute(value, axis, [(i, i ^ distance) for i in range(count)])
        value = value + partner
        distance *= 2
    return value


def one_hot_skew(block_width, tap_span):
    shape = (tap_span, block_width, block_width)
    d = lax.broadcasted_iota(jnp.int32, shape, 0)
    m = lax.broadcasted_iota(jnp.int32, shape, 1)
    i = lax.broadcasted_iota(jnp.int32, shape, 2)
    hit = d == i - m + (block_width - 1)
    return jnp.where(hit, 1.0, 0.0).astype(jnp.bfloat16).reshape(tap_span, block_width * block_width)


def toeplitz(kernel_taps, block_width, skew):
    atoms_here, tap_count = kernel_taps.shape
    zero_pad = jnp.zeros((atoms_here, block_width), kernel_taps.dtype)
    padded = jnp.concatenate([zero_pad, kernel_taps, zero_pad, zero_pad], axis=1)
    lag_blocks = tap_count // block_width
    tap_span = 2 * block_width
    bands = jnp.concatenate(
        [padded[:, off * block_width + 1 : off * block_width + 1 + tap_span] for off in range(lag_blocks + 1)],
        axis=0,
    )
    flat = jnp.dot(bands, skew, preferred_element_type=jnp.float32).astype(kernel_taps.dtype)
    flat = flat.reshape(lag_blocks + 1, atoms_here, block_width, block_width)
    return [flat[off] for off in range(lag_blocks + 1)]


def lag_sums(code_ext, others, block_width, tap_count, skew):
    atoms_here, seg_len = others.shape
    block_count = seg_len // block_width
    lag_blocks = tap_count // block_width
    extended = code_ext.reshape(atoms_here, block_count + lag_blocks, block_width)
    others_blocks = others.reshape(atoms_here, block_count, block_width)
    grads = []
    for offset in range(lag_blocks + 1):
        window = extended[:, lag_blocks - offset : lag_blocks - offset + block_count]
        grads.append(
            jnp.einsum(
                "kbm,kbi->kmi", window, others_blocks, preferred_element_type=jnp.float32, precision=highest
            )
        )
    stacked = jnp.concatenate(grads, axis=0).reshape((lag_blocks + 1) * atoms_here, block_width * block_width)
    bands = jnp.dot(stacked, skew.astype(jnp.float32).T, precision=highest)
    bands = bands.reshape(lag_blocks + 1, atoms_here, 2 * block_width)
    total = jnp.zeros((atoms_here, tap_count + 3 * block_width), jnp.float32)
    for offset in range(lag_blocks + 1):
        start = offset * block_width + 1
        total = total.at[:, start : start + 2 * block_width].add(bands[offset])
    return total[:, block_width : block_width + tap_count]


def convolve_blocks(matrices, code_rows, before, block_width):
    atoms_here, seg_len = code_rows.shape
    block_count = seg_len // block_width
    lag_blocks = len(matrices) - 1
    extended = jnp.concatenate([before, code_rows], axis=1).reshape(
        atoms_here, block_count + lag_blocks, block_width
    )
    summed = jnp.zeros((atoms_here, block_count, block_width), jnp.float32)
    for offset, matrix in enumerate(matrices):
        window = extended[:, lag_blocks - offset : lag_blocks - offset + block_count]
        summed = summed + jnp.einsum(
            "kbm,kmi->kbi", window, matrix, preferred_element_type=jnp.float32, precision=highest
        )
    return summed.reshape(atoms_here, seg_len)


def correlate_blocks(matrices, residual_b, after_rim, block_width):
    atoms_here, seg_len = residual_b.shape
    block_count = seg_len // block_width
    extended = jnp.concatenate([residual_b, after_rim], axis=1).reshape(
        atoms_here, block_count + len(matrices) - 1, block_width
    )
    summed = jnp.zeros((atoms_here, block_count, block_width), jnp.float32)
    for offset, matrix in enumerate(matrices):
        window = extended[:, offset : offset + block_count]
        summed = summed + jnp.einsum(
            "kbi,kmi->kbm", window, matrix, preferred_element_type=jnp.float32, precision=highest
        )
    return summed.reshape(atoms_here, seg_len)


def reconstruct(matrices, latent_rows, block_width, tap_count):
    latent_b = latent_rows.astype(jnp.bfloat16)
    before = passed_along(latent_b[:, latent_b.shape[1] - tap_count :], "seg", 1)
    return (convolve_blocks(matrices, latent_b, before, block_width), before, latent_b)


def on_device(signal, spatial, temporal, start_codes, thresholds, step_sizes, breaks):
    chan_rows, seg_len = signal.shape
    atoms_all, tap_count = temporal.shape
    block_width = 128
    skew = one_hot_skew(block_width, 2 * block_width)
    positions = lax.axis_index("seg") * seg_len + lax.iota(jnp.int32, seg_len)
    crosses = (positions[None, :] < breaks[:, None]) & (
        breaks[:, None] < positions[None, :] + tap_count
    )
    allowed = jnp.where(jnp.any(crosses, axis=0), 0.0, 1.0).astype(jnp.float32)
    raw_start = butterfly_sum(jnp.dot(spatial.T, spatial, precision=highest), "chan")
    scaling = 1.0 / jnp.sqrt(jnp.diag(raw_start) + epsilon)
    space_loc = spatial * scaling[None, :]
    gram_matrix = raw_start * scaling[:, None] * scaling[None, :]
    kernel = temporal / jnp.sqrt(jnp.sum(temporal * temporal, axis=1, keepdims=True) + epsilon)
    latent = start_codes
    for sweep_index in range(OUTER):
        space_b = space_loc.astype(jnp.bfloat16)
        kernel_b = kernel.astype(jnp.bfloat16)
        projected = butterfly_sum(
            jnp.dot(space_b.T, signal, preferred_element_type=jnp.float32), "chan"
        )
        own_gram = gram_matrix

        def mix_atoms(rebuilt_part):
            return jnp.dot(own_gram, rebuilt_part, precision=highest)

        matrices = toeplitz(kernel_b, block_width, skew)
        step_col = step_sizes[:, None]
        limit_col = (step_sizes * thresholds)[:, None]

        def shrink_step(iteration, current):
            rebuilt, _, _ = reconstruct(matrices, current, block_width, tap_count)
            residual = projected - mix_atoms(rebuilt)
            residual_b = residual.astype(jnp.bfloat16)
            after_rim = passed_along(residual_b[:, :tap_count], "seg", -1)
            descent = correlate_blocks(matrices, residual_b, after_rim, block_width)
            stepped = current + step_col * descent
            return (
                allowed[None, :]
                * jnp.sign(stepped)
                * jnp.maximum(jnp.abs(stepped) - limit_col, 0.0)
            )

        latent = lax.fori_loop(0, ITERS, shrink_step, latent)
        rebuilt, before, latent_b = reconstruct(matrices, latent, block_width, tap_count)
        rebuilt_b = rebuilt.astype(jnp.bfloat16)
        row_part = jnp.dot(signal, rebuilt_b.T, preferred_element_type=jnp.float32)
        others = projected - jnp.dot(
            gram_matrix - jnp.diag(jnp.diag(gram_matrix)), rebuilt, precision=highest
        )
        code_ext = jnp.concatenate([before, latent_b], axis=1)
        taps_part = lag_sums(code_ext, others, block_width, tap_count, skew)
        cross_part = jnp.dot(rebuilt, rebuilt.T, precision=highest)
        joined = butterfly_sum(jnp.concatenate([row_part, cross_part, taps_part.T], axis=0), "seg")
        stats_rows = joined[:chan_rows]
        cross_gram = joined[chan_rows : chan_rows + atoms_all]
        raw_kernel = joined[chan_rows + atoms_all :].T
        raw_rows = stats_rows - jnp.dot(
            space_loc, cross_gram - jnp.diag(jnp.diag(cross_gram)), precision=highest
        )
        raw_gram = butterfly_sum(jnp.dot(raw_rows.T, raw_rows, precision=highest), "chan")
        scaling = 1.0 / jnp.sqrt(jnp.diag(raw_gram) + epsilon)
        space_loc = raw_rows * scaling[None, :]
        gram_matrix = raw_gram * scaling[:, None] * scaling[None, :]
        kernel = raw_kernel / jnp.sqrt(
            jnp.sum(raw_kernel * raw_kernel, axis=1, keepdims=True) + epsilon
        )
    return (latent, space_loc, kernel)


def solution(mesh):
    placed = (P("chan", "seg"), P("chan", None), P(), P(None, "seg"), P(), P(), P())
    return jax.shard_map(
        on_device,
        mesh=mesh,
        in_specs=placed,
        out_specs=(P(None, "seg"), P("chan", None), P()),
        check_vma=False,
    )
```

```python
import jax
import jax.numpy as jnp
from jax import lax
from jax.sharding import PartitionSpec as P

ITERS = 10
OUTER = 2
CHUNK = 5
GHOST_BLOCKS = 10


epsilon = 1e-06
highest = lax.Precision.HIGHEST


def passed_along(value, axis, steps):
    count = lax.axis_size(axis)
    leading, last = (max(0, -steps), min(count, count - steps))
    return lax.ppermute(value, axis, [(source, source + steps) for source in range(leading, last)])


def widened(rows, ghost):
    seg_len = rows.shape[1]
    from_left = passed_along(rows[:, seg_len - ghost :], "seg", 1)
    from_right = passed_along(rows[:, :ghost], "seg", -1)
    return jnp.concatenate([from_left, rows, from_right], axis=1)


def butterfly_sum(value, axis):
    count = lax.axis_size(axis)
    distance = 1
    while distance < count:
        partner = lax.ppermute(value, axis, [(i, i ^ distance) for i in range(count)])
        value = value + partner
        distance *= 2
    return value


def one_hot_skew(block_width, tap_span):
    shape = (tap_span, block_width, block_width)
    d = lax.broadcasted_iota(jnp.int32, shape, 0)
    m = lax.broadcasted_iota(jnp.int32, shape, 1)
    i = lax.broadcasted_iota(jnp.int32, shape, 2)
    hit = d == i - m + (block_width - 1)
    return jnp.where(hit, 1.0, 0.0).astype(jnp.bfloat16).reshape(tap_span, block_width * block_width)


def toeplitz(kernel_taps, block_width, skew):
    atoms_here, tap_count = kernel_taps.shape
    zero_pad = jnp.zeros((atoms_here, block_width), kernel_taps.dtype)
    padded = jnp.concatenate([zero_pad, kernel_taps, zero_pad, zero_pad], axis=1)
    lag_blocks = tap_count // block_width
    tap_span = 2 * block_width
    bands = jnp.concatenate(
        [padded[:, off * block_width + 1 : off * block_width + 1 + tap_span] for off in range(lag_blocks + 1)],
        axis=0,
    )
    flat = jnp.dot(bands, skew, preferred_element_type=jnp.float32).astype(kernel_taps.dtype)
    flat = flat.reshape(lag_blocks + 1, atoms_here, block_width, block_width)
    return [flat[off] for off in range(lag_blocks + 1)]


def lag_sums(code_ext, others, block_width, tap_count, skew):
    atoms_here, seg_len = others.shape
    block_count = seg_len // block_width
    lag_blocks = tap_count // block_width
    extended = code_ext.reshape(atoms_here, block_count + lag_blocks, block_width)
    others_blocks = others.reshape(atoms_here, block_count, block_width)
    grads = []
    for offset in range(lag_blocks + 1):
        window = extended[:, lag_blocks - offset : lag_blocks - offset + block_count]
        grads.append(
            jnp.einsum(
                "kbm,kbi->kmi", window, others_blocks, preferred_element_type=jnp.float32, precision=highest
            )
        )
    stacked = jnp.concatenate(grads, axis=0).reshape((lag_blocks + 1) * atoms_here, block_width * block_width)
    bands = jnp.dot(stacked, skew.astype(jnp.float32).T, precision=highest)
    bands = bands.reshape(lag_blocks + 1, atoms_here, 2 * block_width)
    total = jnp.zeros((atoms_here, tap_count + 3 * block_width), jnp.float32)
    for offset in range(lag_blocks + 1):
        start = offset * block_width + 1
        total = total.at[:, start : start + 2 * block_width].add(bands[offset])
    return total[:, block_width : block_width + tap_count]


def convolve_blocks(matrices, code_rows, before, block_width):
    atoms_here, seg_len = code_rows.shape
    block_count = seg_len // block_width
    lag_blocks = len(matrices) - 1
    extended = jnp.concatenate([before, code_rows], axis=1).reshape(
        atoms_here, block_count + lag_blocks, block_width
    )
    summed = jnp.zeros((atoms_here, block_count, block_width), jnp.float32)
    for offset, matrix in enumerate(matrices):
        window = extended[:, lag_blocks - offset : lag_blocks - offset + block_count]
        summed = summed + jnp.einsum(
            "kbm,kmi->kbi", window, matrix, preferred_element_type=jnp.float32, precision=highest
        )
    return summed.reshape(atoms_here, seg_len)


def correlate_blocks(matrices, residual_b, after_rim, block_width):
    atoms_here, seg_len = residual_b.shape
    block_count = seg_len // block_width
    extended = jnp.concatenate([residual_b, after_rim], axis=1).reshape(
        atoms_here, block_count + len(matrices) - 1, block_width
    )
    summed = jnp.zeros((atoms_here, block_count, block_width), jnp.float32)
    for offset, matrix in enumerate(matrices):
        window = extended[:, offset : offset + block_count]
        summed = summed + jnp.einsum(
            "kbi,kmi->kbm", window, matrix, preferred_element_type=jnp.float32, precision=highest
        )
    return summed.reshape(atoms_here, seg_len)


def reconstruct(matrices, latent_rows, block_width, tap_count):
    latent_b = latent_rows.astype(jnp.bfloat16)
    before = passed_along(latent_b[:, latent_b.shape[1] - tap_count :], "seg", 1)
    return (convolve_blocks(matrices, latent_b, before, block_width), before, latent_b)


def on_device(signal, spatial, temporal, start_codes, thresholds, step_sizes, breaks):
    chan_rows, seg_len = signal.shape
    atoms_all, tap_count = temporal.shape
    block_width = 128
    skew = one_hot_skew(block_width, 2 * block_width)
    ghost = GHOST_BLOCKS * block_width
    wide_positions = lax.axis_index("seg") * seg_len - ghost + lax.iota(jnp.int32, seg_len + 2 * ghost)
    wide_crosses = (wide_positions[None, :] < breaks[:, None]) & (
        breaks[:, None] < wide_positions[None, :] + tap_count
    )
    inside = jnp.where(
        (wide_positions >= 0) & (wide_positions < seg_len * lax.axis_size("seg")), 1.0, 0.0
    ).astype(jnp.float32)
    allowed_wide = inside * jnp.where(jnp.any(wide_crosses, axis=0), 0.0, 1.0).astype(jnp.float32)
    zero_rim = jnp.zeros((atoms_all, tap_count), jnp.bfloat16)
    raw_start = butterfly_sum(jnp.dot(spatial.T, spatial, precision=highest), "chan")
    scaling = 1.0 / jnp.sqrt(jnp.diag(raw_start) + epsilon)
    space_loc = spatial * scaling[None, :]
    gram_matrix = raw_start * scaling[:, None] * scaling[None, :]
    kernel = temporal / jnp.sqrt(jnp.sum(temporal * temporal, axis=1, keepdims=True) + epsilon)
    latent = start_codes
    for sweep_index in range(OUTER):
        space_b = space_loc.astype(jnp.bfloat16)
        kernel_b = kernel.astype(jnp.bfloat16)
        projected = butterfly_sum(
            jnp.dot(space_b.T, signal, preferred_element_type=jnp.float32), "chan"
        )
        own_gram = gram_matrix

        def mix_atoms(rebuilt_part):
            return jnp.dot(own_gram, rebuilt_part, precision=highest)

        matrices = toeplitz(kernel_b, block_width, skew)
        step_col = step_sizes[:, None]
        limit_col = (step_sizes * thresholds)[:, None]

        projected_wide = widened(projected, ghost)

        def shrink_step(iteration, current):
            rebuilt = convolve_blocks(matrices, current.astype(jnp.bfloat16), zero_rim, block_width)
            residual = (projected_wide - mix_atoms(rebuilt)) * inside[None, :]
            descent = correlate_blocks(matrices, residual.astype(jnp.bfloat16), zero_rim, block_width)
            stepped = current + step_col * descent
            return (
                allowed_wide[None, :]
                * jnp.sign(stepped)
                * jnp.maximum(jnp.abs(stepped) - limit_col, 0.0)
            )

        for chunk in range(ITERS // CHUNK):
            wide = lax.fori_loop(0, CHUNK, shrink_step, widened(latent, ghost))
            latent = wide[:, ghost : ghost + seg_len]
        rebuilt, before, latent_b = reconstruct(matrices, latent, block_width, tap_count)
        rebuilt_b = rebuilt.astype(jnp.bfloat16)
        row_part = jnp.dot(signal, rebuilt_b.T, preferred_element_type=jnp.float32)
        others = projected - jnp.dot(
            gram_matrix - jnp.diag(jnp.diag(gram_matrix)), rebuilt, precision=highest
        )
        code_ext = jnp.concatenate([before, latent_b], axis=1)
        taps_part = lag_sums(code_ext, others, block_width, tap_count, skew)
        cross_part = jnp.dot(rebuilt, rebuilt.T, precision=highest)
        joined = butterfly_sum(jnp.concatenate([row_part, cross_part, taps_part.T], axis=0), "seg")
        stats_rows = joined[:chan_rows]
        cross_gram = joined[chan_rows : chan_rows + atoms_all]
        raw_kernel = joined[chan_rows + atoms_all :].T
        raw_rows = stats_rows - jnp.dot(
            space_loc, cross_gram - jnp.diag(jnp.diag(cross_gram)), precision=highest
        )
        raw_gram = butterfly_sum(jnp.dot(raw_rows.T, raw_rows, precision=highest), "chan")
        scaling = 1.0 / jnp.sqrt(jnp.diag(raw_gram) + epsilon)
        space_loc = raw_rows * scaling[None, :]
        gram_matrix = raw_gram * scaling[:, None] * scaling[None, :]
        kernel = raw_kernel / jnp.sqrt(
            jnp.sum(raw_kernel * raw_kernel, axis=1, keepdims=True) + epsilon
        )
    return (latent, space_loc, kernel)


def solution(mesh):
    placed = (P("chan", "seg"), P("chan", None), P(), P(None, "seg"), P(), P(), P())
    return jax.shard_map(
        on_device,
        mesh=mesh,
        in_specs=placed,
        out_specs=(P(None, "seg"), P("chan", None), P()),
        check_vma=False,
    )
```

```python
import jax
import jax.numpy as jnp
from jax import lax
from jax.sharding import PartitionSpec as P

ITERS = 10
OUTER = 2
CHUNK = 5
GHOST_BLOCKS = 10


epsilon = 1e-06
highest = lax.Precision.HIGHEST


def passed_along(value, axis, steps):
    count = lax.axis_size(axis)
    leading, last = (max(0, -steps), min(count, count - steps))
    return lax.ppermute(value, axis, [(source, source + steps) for source in range(leading, last)])


def widened(rows, ghost):
    seg_len = rows.shape[1]
    from_left = passed_along(rows[:, seg_len - ghost :], "seg", 1)
    from_right = passed_along(rows[:, :ghost], "seg", -1)
    return jnp.concatenate([from_left, rows, from_right], axis=1)


def butterfly_sum(value, axis):
    count = lax.axis_size(axis)
    distance = 1
    while distance < count:
        partner = lax.ppermute(value, axis, [(i, i ^ distance) for i in range(count)])
        value = value + partner
        distance *= 2
    return value


def one_hot_skew(block_width, tap_span):
    shape = (tap_span, block_width, block_width)
    d = lax.broadcasted_iota(jnp.int32, shape, 0)
    m = lax.broadcasted_iota(jnp.int32, shape, 1)
    i = lax.broadcasted_iota(jnp.int32, shape, 2)
    hit = d == i - m + (block_width - 1)
    return jnp.where(hit, 1.0, 0.0).astype(jnp.bfloat16).reshape(tap_span, block_width * block_width)


def toeplitz(kernel_taps, block_width, skew):
    atoms_here, tap_count = kernel_taps.shape
    zero_pad = jnp.zeros((atoms_here, block_width), kernel_taps.dtype)
    padded = jnp.concatenate([zero_pad, kernel_taps, zero_pad, zero_pad], axis=1)
    lag_blocks = tap_count // block_width
    tap_span = 2 * block_width
    bands = jnp.concatenate(
        [padded[:, off * block_width + 1 : off * block_width + 1 + tap_span] for off in range(lag_blocks + 1)],
        axis=0,
    )
    flat = jnp.dot(bands, skew, preferred_element_type=jnp.float32).astype(kernel_taps.dtype)
    flat = flat.reshape(lag_blocks + 1, atoms_here, block_width, block_width)
    return [flat[off] for off in range(lag_blocks + 1)]


def lag_sums(code_ext, others, block_width, tap_count, skew):
    atoms_here, seg_len = others.shape
    block_count = seg_len // block_width
    lag_blocks = tap_count // block_width
    extended = code_ext.reshape(atoms_here, block_count + lag_blocks, block_width)
    others_blocks = others.reshape(atoms_here, block_count, block_width)
    grads = []
    for offset in range(lag_blocks + 1):
        window = extended[:, lag_blocks - offset : lag_blocks - offset + block_count]
        grads.append(
            jnp.einsum(
                "kbm,kbi->kmi", window, others_blocks, preferred_element_type=jnp.float32, precision=highest
            )
        )
    stacked = jnp.concatenate(grads, axis=0).reshape((lag_blocks + 1) * atoms_here, block_width * block_width)
    pieces = []
    rest = stacked
    for _ in range(3):
        piece = rest.astype(jnp.bfloat16)
        pieces.append(piece)
        rest = rest - piece.astype(jnp.float32)
    split = jnp.concatenate(pieces, axis=0)
    bands = jnp.dot(split, skew.T, preferred_element_type=jnp.float32)
    bands = bands.reshape(3, (lag_blocks + 1) * atoms_here, 2 * block_width)
    bands = (bands[0] + bands[1] + bands[2]).reshape(lag_blocks + 1, atoms_here, 2 * block_width)
    total = jnp.zeros((atoms_here, tap_count + 3 * block_width), jnp.float32)
    for offset in range(lag_blocks + 1):
        start = offset * block_width + 1
        total = total.at[:, start : start + 2 * block_width].add(bands[offset])
    return total[:, block_width : block_width + tap_count]


def convolve_blocks(matrices, code_rows, before, block_width):
    atoms_here, seg_len = code_rows.shape
    block_count = seg_len // block_width
    lag_blocks = len(matrices) - 1
    extended = jnp.concatenate([before, code_rows], axis=1).reshape(
        atoms_here, block_count + lag_blocks, block_width
    )
    summed = jnp.zeros((atoms_here, block_count, block_width), jnp.float32)
    for offset, matrix in enumerate(matrices):
        window = extended[:, lag_blocks - offset : lag_blocks - offset + block_count]
        summed = summed + jnp.einsum(
            "kbm,kmi->kbi", window, matrix, preferred_element_type=jnp.float32, precision=highest
        )
    return summed.reshape(atoms_here, seg_len)


def correlate_blocks(matrices, residual_b, after_rim, block_width):
    atoms_here, seg_len = residual_b.shape
    block_count = seg_len // block_width
    extended = jnp.concatenate([residual_b, after_rim], axis=1).reshape(
        atoms_here, block_count + len(matrices) - 1, block_width
    )
    summed = jnp.zeros((atoms_here, block_count, block_width), jnp.float32)
    for offset, matrix in enumerate(matrices):
        window = extended[:, offset : offset + block_count]
        summed = summed + jnp.einsum(
            "kbi,kim->kbm", window, matrix, preferred_element_type=jnp.float32, precision=highest
        )
    return summed.reshape(atoms_here, seg_len)


def reconstruct(matrices, latent_rows, block_width, tap_count):
    latent_b = latent_rows.astype(jnp.bfloat16)
    before = passed_along(latent_b[:, latent_b.shape[1] - tap_count :], "seg", 1)
    return (convolve_blocks(matrices, latent_b, before, block_width), before, latent_b)


def on_device(signal, spatial, temporal, start_codes, thresholds, step_sizes, breaks):
    chan_rows, seg_len = signal.shape
    atoms_all, tap_count = temporal.shape
    block_width = 128
    skew = one_hot_skew(block_width, 2 * block_width)
    ghost = GHOST_BLOCKS * block_width
    wide_positions = lax.axis_index("seg") * seg_len - ghost + lax.iota(jnp.int32, seg_len + 2 * ghost)
    wide_crosses = (wide_positions[None, :] < breaks[:, None]) & (
        breaks[:, None] < wide_positions[None, :] + tap_count
    )
    inside = jnp.where(
        (wide_positions >= 0) & (wide_positions < seg_len * lax.axis_size("seg")), 1.0, 0.0
    ).astype(jnp.float32)
    allowed_wide = inside * jnp.where(jnp.any(wide_crosses, axis=0), 0.0, 1.0).astype(jnp.float32)
    zero_rim = jnp.zeros((atoms_all, tap_count), jnp.bfloat16)
    raw_start = butterfly_sum(jnp.dot(spatial.T, spatial, precision=highest), "chan")
    scaling = 1.0 / jnp.sqrt(jnp.diag(raw_start) + epsilon)
    space_loc = spatial * scaling[None, :]
    gram_matrix = raw_start * scaling[:, None] * scaling[None, :]
    kernel = temporal / jnp.sqrt(jnp.sum(temporal * temporal, axis=1, keepdims=True) + epsilon)
    latent = start_codes
    for sweep_index in range(OUTER):
        space_b = space_loc.astype(jnp.bfloat16)
        kernel_b = kernel.astype(jnp.bfloat16)
        projected = butterfly_sum(
            jnp.dot(space_b.T, signal, preferred_element_type=jnp.float32), "chan"
        )
        own_gram = gram_matrix

        def mix_atoms(rebuilt_part):
            return jnp.dot(own_gram, rebuilt_part, precision=highest)

        matrices = toeplitz(kernel_b, block_width, skew)
        flipped = [jnp.swapaxes(matrix, 1, 2) for matrix in matrices]
        step_col = step_sizes[:, None]
        limit_col = (step_sizes * thresholds)[:, None]

        projected_wide = widened(projected, ghost)

        def shrink_step(iteration, carried):
            current, current_b = carried
            rebuilt = convolve_blocks(matrices, current_b, zero_rim, block_width)
            residual = (projected_wide - mix_atoms(rebuilt)) * inside[None, :]
            descent = correlate_blocks(flipped, residual.astype(jnp.bfloat16), zero_rim, block_width)
            stepped = current + step_col * descent
            shrunk = (
                allowed_wide[None, :]
                * jnp.sign(stepped)
                * jnp.maximum(jnp.abs(stepped) - limit_col, 0.0)
            )
            return (shrunk, shrunk.astype(jnp.bfloat16))

        for chunk in range(ITERS // CHUNK):
            wide = widened(latent, ghost)
            wide, _ = lax.fori_loop(0, CHUNK, shrink_step, (wide, wide.astype(jnp.bfloat16)))
            latent = wide[:, ghost : ghost + seg_len]
        rebuilt, before, latent_b = reconstruct(matrices, latent, block_width, tap_count)
        rebuilt_b = rebuilt.astype(jnp.bfloat16)
        row_part = jnp.dot(signal, rebuilt_b.T, preferred_element_type=jnp.float32)
        others = projected - jnp.dot(
            gram_matrix - jnp.diag(jnp.diag(gram_matrix)), rebuilt, precision=highest
        )
        code_ext = jnp.concatenate([before, latent_b], axis=1)
        taps_part = lag_sums(code_ext, others, block_width, tap_count, skew)
        cross_part = jnp.dot(rebuilt, rebuilt.T, precision=highest)
        joined = butterfly_sum(jnp.concatenate([row_part, cross_part, taps_part.T], axis=0), "seg")
        stats_rows = joined[:chan_rows]
        cross_gram = joined[chan_rows : chan_rows + atoms_all]
        raw_kernel = joined[chan_rows + atoms_all :].T
        raw_rows = stats_rows - jnp.dot(
            space_loc, cross_gram - jnp.diag(jnp.diag(cross_gram)), precision=highest
        )
        raw_gram = butterfly_sum(jnp.dot(raw_rows.T, raw_rows, precision=highest), "chan")
        scaling = 1.0 / jnp.sqrt(jnp.diag(raw_gram) + epsilon)
        space_loc = raw_rows * scaling[None, :]
        gram_matrix = raw_gram * scaling[:, None] * scaling[None, :]
        kernel = raw_kernel / jnp.sqrt(
            jnp.sum(raw_kernel * raw_kernel, axis=1, keepdims=True) + epsilon
        )
    return (latent, space_loc, kernel)


def solution(mesh):
    placed = (P("chan", "seg"), P("chan", None), P(), P(None, "seg"), P(), P(), P())
    return jax.shard_map(
        on_device,
        mesh=mesh,
        in_specs=placed,
        out_specs=(P(None, "seg"), P("chan", None), P()),
        check_vma=False,
    )
```

```python
import jax
import jax.numpy as jnp
from jax import lax
from jax.sharding import PartitionSpec as P

ITERS = 10
OUTER = 2
CHUNK = 5
GHOST_BLOCKS = 10


epsilon = 1e-06
highest = lax.Precision.HIGHEST


def passed_along(value, axis, steps):
    count = lax.axis_size(axis)
    leading, last = (max(0, -steps), min(count, count - steps))
    return lax.ppermute(value, axis, [(source, source + steps) for source in range(leading, last)])


def widened(rows, ghost):
    seg_len = rows.shape[1]
    from_left = passed_along(rows[:, seg_len - ghost :], "seg", 1)
    from_right = passed_along(rows[:, :ghost], "seg", -1)
    return jnp.concatenate([from_left, rows, from_right], axis=1)


def butterfly_sum(value, axis):
    count = lax.axis_size(axis)
    distance = 1
    while distance < count:
        partner = lax.ppermute(value, axis, [(i, i ^ distance) for i in range(count)])
        value = value + partner
        distance *= 2
    return value


def one_hot_skew(block_width, tap_span, transposed=False):
    shape = (tap_span, block_width, block_width)
    d = lax.broadcasted_iota(jnp.int32, shape, 0)
    m = lax.broadcasted_iota(jnp.int32, shape, 2 if transposed else 1)
    i = lax.broadcasted_iota(jnp.int32, shape, 1 if transposed else 2)
    hit = d == i - m + (block_width - 1)
    return jnp.where(hit, 1.0, 0.0).astype(jnp.bfloat16).reshape(tap_span, block_width * block_width)


def band_sums_matrix(block_width, tap_span):
    shape = (block_width, block_width, tap_span)
    m = lax.broadcasted_iota(jnp.int32, shape, 0)
    i = lax.broadcasted_iota(jnp.int32, shape, 1)
    d = lax.broadcasted_iota(jnp.int32, shape, 2)
    hit = d == i - m + (block_width - 1)
    return jnp.where(hit, 1.0, 0.0).reshape(block_width * block_width, tap_span)


def toeplitz(kernel_taps, block_width, skew):
    atoms_here, tap_count = kernel_taps.shape
    zero_pad = jnp.zeros((atoms_here, block_width), kernel_taps.dtype)
    padded = jnp.concatenate([zero_pad, kernel_taps, zero_pad, zero_pad], axis=1)
    lag_blocks = tap_count // block_width
    tap_span = 2 * block_width
    bands = jnp.concatenate(
        [padded[:, off * block_width + 1 : off * block_width + 1 + tap_span] for off in range(lag_blocks + 1)],
        axis=0,
    )
    flat = jnp.dot(bands, skew, preferred_element_type=jnp.float32).astype(kernel_taps.dtype)
    flat = flat.reshape(lag_blocks + 1, atoms_here, block_width, block_width)
    return [flat[off] for off in range(lag_blocks + 1)]


def lag_sums(code_ext, others, block_width, tap_count):
    atoms_here, seg_len = others.shape
    block_count = seg_len // block_width
    lag_blocks = tap_count // block_width
    extended = code_ext.reshape(atoms_here, block_count + lag_blocks, block_width)
    others_blocks = others.reshape(atoms_here, block_count, block_width)
    grads = []
    for offset in range(lag_blocks + 1):
        window = extended[:, lag_blocks - offset : lag_blocks - offset + block_count]
        grads.append(
            jnp.einsum(
                "kbm,kbi->kmi", window, others_blocks, preferred_element_type=jnp.float32, precision=highest
            )
        )
    stacked = jnp.concatenate(grads, axis=0).reshape((lag_blocks + 1) * atoms_here, block_width * block_width)
    bands = jnp.dot(stacked, band_sums_matrix(block_width, 2 * block_width), precision=lax.Precision.HIGH)
    bands = bands.reshape(lag_blocks + 1, atoms_here, 2 * block_width)
    total = jnp.zeros((atoms_here, tap_count + 3 * block_width), jnp.float32)
    for offset in range(lag_blocks + 1):
        start = offset * block_width + 1
        total = total.at[:, start : start + 2 * block_width].add(bands[offset])
    return total[:, block_width : block_width + tap_count]


def convolve_blocks(matrices, code_rows, before, block_width):
    atoms_here, seg_len = code_rows.shape
    block_count = seg_len // block_width
    lag_blocks = len(matrices) - 1
    extended = jnp.concatenate([before, code_rows], axis=1).reshape(
        atoms_here, block_count + lag_blocks, block_width
    )
    summed = jnp.zeros((atoms_here, block_count, block_width), jnp.float32)
    for offset, matrix in enumerate(matrices):
        window = extended[:, lag_blocks - offset : lag_blocks - offset + block_count]
        summed = summed + jnp.einsum(
            "kbm,kmi->kbi", window, matrix, preferred_element_type=jnp.float32, precision=highest
        )
    return summed.reshape(atoms_here, seg_len)


def correlate_blocks(matrices, residual_b, after_rim, block_width):
    atoms_here, seg_len = residual_b.shape
    block_count = seg_len // block_width
    extended = jnp.concatenate([residual_b, after_rim], axis=1).reshape(
        atoms_here, block_count + len(matrices) - 1, block_width
    )
    summed = jnp.zeros((atoms_here, block_count, block_width), jnp.float32)
    for offset, matrix in enumerate(matrices):
        window = extended[:, offset : offset + block_count]
        summed = summed + jnp.einsum(
            "kbi,kim->kbm", window, matrix, preferred_element_type=jnp.float32, precision=highest
        )
    return summed.reshape(atoms_here, seg_len)


def reconstruct(matrices, latent_rows, block_width, tap_count):
    latent_b = latent_rows.astype(jnp.bfloat16)
    before = passed_along(latent_b[:, latent_b.shape[1] - tap_count :], "seg", 1)
    return (convolve_blocks(matrices, latent_b, before, block_width), before, latent_b)


def on_device(signal, spatial, temporal, start_codes, thresholds, step_sizes, breaks):
    chan_rows, seg_len = signal.shape
    atoms_all, tap_count = temporal.shape
    block_width = 128
    skew = one_hot_skew(block_width, 2 * block_width)
    skew_flipped = one_hot_skew(block_width, 2 * block_width, transposed=True)
    ghost = GHOST_BLOCKS * block_width
    wide_positions = lax.axis_index("seg") * seg_len - ghost + lax.iota(jnp.int32, seg_len + 2 * ghost)
    wide_crosses = (wide_positions[None, :] < breaks[:, None]) & (
        breaks[:, None] < wide_positions[None, :] + tap_count
    )
    inside = jnp.where(
        (wide_positions >= 0) & (wide_positions < seg_len * lax.axis_size("seg")), 1.0, 0.0
    ).astype(jnp.float32)
    allowed_wide = inside * jnp.where(jnp.any(wide_crosses, axis=0), 0.0, 1.0).astype(jnp.float32)
    zero_rim = jnp.zeros((atoms_all, tap_count), jnp.bfloat16)
    raw_start = butterfly_sum(jnp.dot(spatial.T, spatial, precision=highest), "chan")
    scaling = 1.0 / jnp.sqrt(jnp.diag(raw_start) + epsilon)
    space_loc = spatial * scaling[None, :]
    gram_matrix = raw_start * scaling[:, None] * scaling[None, :]
    kernel = temporal / jnp.sqrt(jnp.sum(temporal * temporal, axis=1, keepdims=True) + epsilon)
    latent = start_codes
    for sweep_index in range(OUTER):
        space_b = space_loc.astype(jnp.bfloat16)
        kernel_b = kernel.astype(jnp.bfloat16)
        projected = butterfly_sum(
            jnp.dot(space_b.T, signal, preferred_element_type=jnp.float32), "chan"
        )
        own_gram = gram_matrix

        def mix_atoms(rebuilt_part):
            return jnp.dot(own_gram, rebuilt_part, precision=highest)

        matrices = toeplitz(kernel_b, block_width, skew)
        flipped = toeplitz(kernel_b, block_width, skew_flipped)
        step_col = step_sizes[:, None]
        limit_col = (step_sizes * thresholds)[:, None]

        projected_wide = widened(projected, ghost)

        def shrink_step(iteration, carried):
            current, current_b = carried
            rebuilt = convolve_blocks(matrices, current_b, zero_rim, block_width)
            residual = (projected_wide - mix_atoms(rebuilt)) * inside[None, :]
            descent = correlate_blocks(flipped, residual.astype(jnp.bfloat16), zero_rim, block_width)
            stepped = current + step_col * descent
            shrunk = (
                allowed_wide[None, :]
                * jnp.sign(stepped)
                * jnp.maximum(jnp.abs(stepped) - limit_col, 0.0)
            )
            return (shrunk, shrunk.astype(jnp.bfloat16))

        for chunk in range(ITERS // CHUNK):
            wide = widened(latent, ghost)
            wide, _ = lax.fori_loop(0, CHUNK, shrink_step, (wide, wide.astype(jnp.bfloat16)))
            latent = wide[:, ghost : ghost + seg_len]
        rebuilt, before, latent_b = reconstruct(matrices, latent, block_width, tap_count)
        rebuilt_b = rebuilt.astype(jnp.bfloat16)
        row_part = jnp.dot(signal, rebuilt_b.T, preferred_element_type=jnp.float32)
        others = projected - jnp.dot(
            gram_matrix - jnp.diag(jnp.diag(gram_matrix)), rebuilt, precision=highest
        )
        code_ext = jnp.concatenate([before, latent_b], axis=1)
        taps_part = lag_sums(code_ext, others, block_width, tap_count)
        cross_part = jnp.dot(rebuilt, rebuilt.T, precision=highest)
        joined = butterfly_sum(jnp.concatenate([row_part, cross_part, taps_part.T], axis=0), "seg")
        stats_rows = joined[:chan_rows]
        cross_gram = joined[chan_rows : chan_rows + atoms_all]
        raw_kernel = joined[chan_rows + atoms_all :].T
        raw_rows = stats_rows - jnp.dot(
            space_loc, cross_gram - jnp.diag(jnp.diag(cross_gram)), precision=highest
        )
        raw_gram = butterfly_sum(jnp.dot(raw_rows.T, raw_rows, precision=highest), "chan")
        scaling = 1.0 / jnp.sqrt(jnp.diag(raw_gram) + epsilon)
        space_loc = raw_rows * scaling[None, :]
        gram_matrix = raw_gram * scaling[:, None] * scaling[None, :]
        kernel = raw_kernel / jnp.sqrt(
            jnp.sum(raw_kernel * raw_kernel, axis=1, keepdims=True) + epsilon
        )
    return (latent, space_loc, kernel)


def solution(mesh):
    placed = (P("chan", "seg"), P("chan", None), P(), P(None, "seg"), P(), P(), P())
    return jax.shard_map(
        on_device,
        mesh=mesh,
        in_specs=placed,
        out_specs=(P(None, "seg"), P("chan", None), P()),
        check_vma=False,
    )
```

```python
import jax
import jax.numpy as jnp
from jax import lax
from jax.sharding import PartitionSpec as P

ITERS = 10
OUTER = 2
CHUNK = 5
GHOST_BLOCKS = 10


epsilon = 1e-06
highest = lax.Precision.HIGHEST


def passed_along(value, axis, steps):
    count = lax.axis_size(axis)
    leading, last = (max(0, -steps), min(count, count - steps))
    return lax.ppermute(value, axis, [(source, source + steps) for source in range(leading, last)])


def widened(rows, ghost):
    seg_len = rows.shape[1]
    from_left = passed_along(rows[:, seg_len - ghost :], "seg", 1)
    from_right = passed_along(rows[:, :ghost], "seg", -1)
    return jnp.concatenate([from_left, rows, from_right], axis=1)


def butterfly_sum(value, axis):
    count = lax.axis_size(axis)
    distance = 1
    while distance < count:
        partner = lax.ppermute(value, axis, [(i, i ^ distance) for i in range(count)])
        value = value + partner
        distance *= 2
    return value


def one_hot_skew(block_width, tap_span, transposed=False):
    shape = (tap_span, block_width, block_width)
    d = lax.broadcasted_iota(jnp.int32, shape, 0)
    m = lax.broadcasted_iota(jnp.int32, shape, 2 if transposed else 1)
    i = lax.broadcasted_iota(jnp.int32, shape, 1 if transposed else 2)
    hit = d == i - m + (block_width - 1)
    return jnp.where(hit, 1.0, 0.0).astype(jnp.bfloat16).reshape(tap_span, block_width * block_width)


def band_sums_matrix(block_width, tap_span):
    shape = (block_width, block_width, tap_span)
    m = lax.broadcasted_iota(jnp.int32, shape, 0)
    i = lax.broadcasted_iota(jnp.int32, shape, 1)
    d = lax.broadcasted_iota(jnp.int32, shape, 2)
    hit = d == i - m + (block_width - 1)
    return jnp.where(hit, 1.0, 0.0).astype(jnp.bfloat16).reshape(block_width * block_width, tap_span)


def toeplitz(kernel_taps, block_width, skew):
    atoms_here, tap_count = kernel_taps.shape
    zero_pad = jnp.zeros((atoms_here, block_width), kernel_taps.dtype)
    padded = jnp.concatenate([zero_pad, kernel_taps, zero_pad, zero_pad], axis=1)
    lag_blocks = tap_count // block_width
    tap_span = 2 * block_width
    bands = jnp.concatenate(
        [padded[:, off * block_width + 1 : off * block_width + 1 + tap_span] for off in range(lag_blocks + 1)],
        axis=0,
    )
    flat = jnp.dot(bands, skew, preferred_element_type=jnp.float32).astype(kernel_taps.dtype)
    flat = flat.reshape(lag_blocks + 1, atoms_here, block_width, block_width)
    return [flat[off] for off in range(lag_blocks + 1)]


def lag_sums(code_ext, others, block_width, tap_count, band_sums):
    atoms_here, seg_len = others.shape
    block_count = seg_len // block_width
    lag_blocks = tap_count // block_width
    extended = code_ext.reshape(atoms_here, block_count + lag_blocks, block_width)
    others_blocks = others.reshape(atoms_here, block_count, block_width)
    grads = []
    for offset in range(lag_blocks + 1):
        window = extended[:, lag_blocks - offset : lag_blocks - offset + block_count]
        grads.append(
            jnp.einsum(
                "kbm,kbi->kmi", window, others_blocks, preferred_element_type=jnp.float32, precision=highest
            )
        )
    stacked = jnp.concatenate(grads, axis=0).reshape((lag_blocks + 1) * atoms_here, block_width * block_width)
    bands = jnp.dot(stacked, band_sums.astype(jnp.float32), precision=lax.Precision.HIGH)
    bands = bands.reshape(lag_blocks + 1, atoms_here, 2 * block_width)
    total = jnp.zeros((atoms_here, tap_count + 3 * block_width), jnp.float32)
    for offset in range(lag_blocks + 1):
        start = offset * block_width + 1
        total = total.at[:, start : start + 2 * block_width].add(bands[offset])
    return total[:, block_width : block_width + tap_count]


def convolve_blocks(matrices, code_rows, before, block_width):
    atoms_here, seg_len = code_rows.shape
    block_count = seg_len // block_width
    lag_blocks = len(matrices) - 1
    extended = jnp.concatenate([before, code_rows], axis=1).reshape(
        atoms_here, block_count + lag_blocks, block_width
    )
    summed = jnp.zeros((atoms_here, block_count, block_width), jnp.float32)
    for offset, matrix in enumerate(matrices):
        window = extended[:, lag_blocks - offset : lag_blocks - offset + block_count]
        summed = summed + jnp.einsum(
            "kbm,kmi->kbi", window, matrix, preferred_element_type=jnp.float32, precision=highest
        )
    return summed.reshape(atoms_here, seg_len)


def correlate_blocks(matrices, residual_b, after_rim, block_width):
    atoms_here, seg_len = residual_b.shape
    block_count = seg_len // block_width
    extended = jnp.concatenate([residual_b, after_rim], axis=1).reshape(
        atoms_here, block_count + len(matrices) - 1, block_width
    )
    summed = jnp.zeros((atoms_here, block_count, block_width), jnp.float32)
    for offset, matrix in enumerate(matrices):
        window = extended[:, offset : offset + block_count]
        summed = summed + jnp.einsum(
            "kbi,kim->kbm", window, matrix, preferred_element_type=jnp.float32, precision=highest
        )
    return summed.reshape(atoms_here, seg_len)


def reconstruct(matrices, latent_rows, block_width, tap_count):
    latent_b = latent_rows.astype(jnp.bfloat16)
    before = passed_along(latent_b[:, latent_b.shape[1] - tap_count :], "seg", 1)
    return (convolve_blocks(matrices, latent_b, before, block_width), before, latent_b)


def on_device(signal, spatial, temporal, start_codes, thresholds, step_sizes, breaks):
    chan_rows, seg_len = signal.shape
    atoms_all, tap_count = temporal.shape
    block_width = 128
    skew = one_hot_skew(block_width, 2 * block_width)
    skew_flipped = one_hot_skew(block_width, 2 * block_width, transposed=True)
    band_sums = lax.optimization_barrier(band_sums_matrix(block_width, 2 * block_width))
    ghost = GHOST_BLOCKS * block_width
    wide_positions = lax.axis_index("seg") * seg_len - ghost + lax.iota(jnp.int32, seg_len + 2 * ghost)
    wide_crosses = (wide_positions[None, :] < breaks[:, None]) & (
        breaks[:, None] < wide_positions[None, :] + tap_count
    )
    inside = jnp.where(
        (wide_positions >= 0) & (wide_positions < seg_len * lax.axis_size("seg")), 1.0, 0.0
    ).astype(jnp.float32)
    allowed_wide = inside * jnp.where(jnp.any(wide_crosses, axis=0), 0.0, 1.0).astype(jnp.float32)
    zero_rim = jnp.zeros((atoms_all, tap_count), jnp.bfloat16)
    raw_start = butterfly_sum(jnp.dot(spatial.T, spatial, precision=highest), "chan")
    scaling = 1.0 / jnp.sqrt(jnp.diag(raw_start) + epsilon)
    space_loc = spatial * scaling[None, :]
    gram_matrix = raw_start * scaling[:, None] * scaling[None, :]
    kernel = temporal / jnp.sqrt(jnp.sum(temporal * temporal, axis=1, keepdims=True) + epsilon)
    latent = start_codes
    for sweep_index in range(OUTER):
        space_b = space_loc.astype(jnp.bfloat16)
        kernel_b = kernel.astype(jnp.bfloat16)
        projected = butterfly_sum(
            jnp.dot(space_b.T, signal, preferred_element_type=jnp.float32), "chan"
        )
        own_gram = gram_matrix

        def mix_atoms(rebuilt_part):
            return jnp.dot(own_gram, rebuilt_part, precision=highest)

        matrices = toeplitz(kernel_b, block_width, skew)
        flipped = toeplitz(kernel_b, block_width, skew_flipped)
        step_col = step_sizes[:, None]
        limit_col = (step_sizes * thresholds)[:, None]

        projected_wide = widened(projected, ghost)

        def shrink_step(iteration, carried):
            current, current_b = carried
            rebuilt = convolve_blocks(matrices, current_b, zero_rim, block_width)
            residual = (projected_wide - mix_atoms(rebuilt)) * inside[None, :]
            descent = correlate_blocks(flipped, residual.astype(jnp.bfloat16), zero_rim, block_width)
            stepped = current + step_col * descent
            shrunk = (
                allowed_wide[None, :]
                * jnp.sign(stepped)
                * jnp.maximum(jnp.abs(stepped) - limit_col, 0.0)
            )
            return (shrunk, shrunk.astype(jnp.bfloat16))

        for chunk in range(ITERS // CHUNK):
            wide = widened(latent, ghost)
            wide, _ = lax.fori_loop(0, CHUNK, shrink_step, (wide, wide.astype(jnp.bfloat16)))
            latent = wide[:, ghost : ghost + seg_len]
        rebuilt, before, latent_b = reconstruct(matrices, latent, block_width, tap_count)
        rebuilt_b = rebuilt.astype(jnp.bfloat16)
        row_part = jnp.dot(signal, rebuilt_b.T, preferred_element_type=jnp.float32)
        others = projected - jnp.dot(
            gram_matrix - jnp.diag(jnp.diag(gram_matrix)), rebuilt, precision=highest
        )
        code_ext = jnp.concatenate([before, latent_b], axis=1)
        taps_part = lag_sums(code_ext, others, block_width, tap_count, band_sums)
        cross_part = jnp.dot(rebuilt, rebuilt.T, precision=highest)
        joined = butterfly_sum(jnp.concatenate([row_part, cross_part, taps_part.T], axis=0), "seg")
        stats_rows = joined[:chan_rows]
        cross_gram = joined[chan_rows : chan_rows + atoms_all]
        raw_kernel = joined[chan_rows + atoms_all :].T
        raw_rows = stats_rows - jnp.dot(
            space_loc, cross_gram - jnp.diag(jnp.diag(cross_gram)), precision=highest
        )
        raw_gram = butterfly_sum(jnp.dot(raw_rows.T, raw_rows, precision=highest), "chan")
        scaling = 1.0 / jnp.sqrt(jnp.diag(raw_gram) + epsilon)
        space_loc = raw_rows * scaling[None, :]
        gram_matrix = raw_gram * scaling[:, None] * scaling[None, :]
        kernel = raw_kernel / jnp.sqrt(
            jnp.sum(raw_kernel * raw_kernel, axis=1, keepdims=True) + epsilon
        )
    return (latent, space_loc, kernel)


def solution(mesh):
    placed = (P("chan", "seg"), P("chan", None), P(), P(None, "seg"), P(), P(), P())
    return jax.shard_map(
        on_device,
        mesh=mesh,
        in_specs=placed,
        out_specs=(P(None, "seg"), P("chan", None), P()),
        check_vma=False,
    )
```

```python
import jax
import jax.numpy as jnp
from jax import lax
from jax.sharding import PartitionSpec as P

ITERS = 10
OUTER = 2
CHUNK = 5
GHOST_BLOCKS = 10


epsilon = 1e-06
highest = lax.Precision.HIGHEST


def passed_along(value, axis, steps):
    count = lax.axis_size(axis)
    leading, last = (max(0, -steps), min(count, count - steps))
    return lax.ppermute(value, axis, [(source, source + steps) for source in range(leading, last)])


def widened(rows, ghost):
    seg_len = rows.shape[1]
    from_left = passed_along(rows[:, seg_len - ghost :], "seg", 1)
    from_right = passed_along(rows[:, :ghost], "seg", -1)
    return jnp.concatenate([from_left, rows, from_right], axis=1)


def butterfly_sum(value, axis):
    count = lax.axis_size(axis)
    distance = 1
    while distance < count:
        partner = lax.ppermute(value, axis, [(i, i ^ distance) for i in range(count)])
        value = value + partner
        distance *= 2
    return value


def one_hot_skew(block_width, tap_span, transposed=False):
    shape = (tap_span, block_width, block_width)
    d = lax.broadcasted_iota(jnp.int32, shape, 0)
    m = lax.broadcasted_iota(jnp.int32, shape, 2 if transposed else 1)
    i = lax.broadcasted_iota(jnp.int32, shape, 1 if transposed else 2)
    hit = d == i - m + (block_width - 1)
    return jnp.where(hit, 1.0, 0.0).astype(jnp.bfloat16).reshape(tap_span, block_width * block_width)


def band_sums_matrix(block_width, tap_count, offset):
    shape = (block_width, block_width, tap_count)
    m = lax.broadcasted_iota(jnp.int32, shape, 0)
    i = lax.broadcasted_iota(jnp.int32, shape, 1)
    tau = lax.broadcasted_iota(jnp.int32, shape, 2)
    hit = tau == i - m + block_width * offset
    return jnp.where(hit, 1.0, 0.0).reshape(block_width * block_width, tap_count)


def toeplitz(kernel_taps, block_width, skew):
    atoms_here, tap_count = kernel_taps.shape
    zero_pad = jnp.zeros((atoms_here, block_width), kernel_taps.dtype)
    padded = jnp.concatenate([zero_pad, kernel_taps, zero_pad, zero_pad], axis=1)
    lag_blocks = tap_count // block_width
    tap_span = 2 * block_width
    bands = jnp.concatenate(
        [padded[:, off * block_width + 1 : off * block_width + 1 + tap_span] for off in range(lag_blocks + 1)],
        axis=0,
    )
    flat = jnp.dot(bands, skew, preferred_element_type=jnp.float32).astype(kernel_taps.dtype)
    flat = flat.reshape(lag_blocks + 1, atoms_here, block_width, block_width)
    return [flat[off] for off in range(lag_blocks + 1)]


def lag_sums(code_ext, others, block_width, tap_count):
    atoms_here, seg_len = others.shape
    block_count = seg_len // block_width
    lag_blocks = tap_count // block_width
    extended = code_ext.reshape(atoms_here, block_count + lag_blocks, block_width)
    others_blocks = others.reshape(atoms_here, block_count, block_width)
    total = jnp.zeros((atoms_here, tap_count), jnp.float32)
    for offset in range(lag_blocks + 1):
        window = extended[:, lag_blocks - offset : lag_blocks - offset + block_count]
        grad = jnp.einsum(
            "kbm,kbi->kmi", window, others_blocks, preferred_element_type=jnp.float32, precision=highest
        ).reshape(atoms_here, block_width * block_width)
        total = total + jnp.dot(grad, band_sums_matrix(block_width, tap_count, offset), precision=highest)
    return total


def convolve_blocks(matrices, code_rows, before, block_width):
    atoms_here, seg_len = code_rows.shape
    block_count = seg_len // block_width
    lag_blocks = len(matrices) - 1
    extended = jnp.concatenate([before, code_rows], axis=1).reshape(
        atoms_here, block_count + lag_blocks, block_width
    )
    summed = jnp.zeros((atoms_here, block_count, block_width), jnp.float32)
    for offset, matrix in enumerate(matrices):
        window = extended[:, lag_blocks - offset : lag_blocks - offset + block_count]
        summed = summed + jnp.einsum(
            "kbm,kmi->kbi", window, matrix, preferred_element_type=jnp.float32, precision=highest
        )
    return summed.reshape(atoms_here, seg_len)


def correlate_blocks(matrices, residual_b, after_rim, block_width):
    atoms_here, seg_len = residual_b.shape
    block_count = seg_len // block_width
    extended = jnp.concatenate([residual_b, after_rim], axis=1).reshape(
        atoms_here, block_count + len(matrices) - 1, block_width
    )
    summed = jnp.zeros((atoms_here, block_count, block_width), jnp.float32)
    for offset, matrix in enumerate(matrices):
        window = extended[:, offset : offset + block_count]
        summed = summed + jnp.einsum(
            "kbi,kim->kbm", window, matrix, preferred_element_type=jnp.float32, precision=highest
        )
    return summed.reshape(atoms_here, seg_len)


def reconstruct(matrices, latent_rows, block_width, tap_count):
    latent_b = latent_rows.astype(jnp.bfloat16)
    before = passed_along(latent_b[:, latent_b.shape[1] - tap_count :], "seg", 1)
    return (convolve_blocks(matrices, latent_b, before, block_width), before, latent_b)


def on_device(signal, spatial, temporal, start_codes, thresholds, step_sizes, breaks):
    chan_rows, seg_len = signal.shape
    atoms_all, tap_count = temporal.shape
    block_width = 128
    skew = one_hot_skew(block_width, 2 * block_width)
    skew_flipped = one_hot_skew(block_width, 2 * block_width, transposed=True)
    ghost = GHOST_BLOCKS * block_width
    wide_positions = lax.axis_index("seg") * seg_len - ghost + lax.iota(jnp.int32, seg_len + 2 * ghost)
    wide_crosses = (wide_positions[None, :] < breaks[:, None]) & (
        breaks[:, None] < wide_positions[None, :] + tap_count
    )
    inside = jnp.where(
        (wide_positions >= 0) & (wide_positions < seg_len * lax.axis_size("seg")), 1.0, 0.0
    ).astype(jnp.float32)
    allowed_wide = inside * jnp.where(jnp.any(wide_crosses, axis=0), 0.0, 1.0).astype(jnp.float32)
    zero_rim = jnp.zeros((atoms_all, tap_count), jnp.bfloat16)
    raw_start = butterfly_sum(jnp.dot(spatial.T, spatial, precision=highest), "chan")
    scaling = 1.0 / jnp.sqrt(jnp.diag(raw_start) + epsilon)
    space_loc = spatial * scaling[None, :]
    gram_matrix = raw_start * scaling[:, None] * scaling[None, :]
    kernel = temporal / jnp.sqrt(jnp.sum(temporal * temporal, axis=1, keepdims=True) + epsilon)
    latent = start_codes
    for sweep_index in range(OUTER):
        space_b = space_loc.astype(jnp.bfloat16)
        kernel_b = kernel.astype(jnp.bfloat16)
        projected = butterfly_sum(
            jnp.dot(space_b.T, signal, preferred_element_type=jnp.float32), "chan"
        )
        own_gram = gram_matrix

        def mix_atoms(rebuilt_part):
            return jnp.dot(own_gram, rebuilt_part, precision=highest)

        matrices = toeplitz(kernel_b, block_width, skew)
        flipped = toeplitz(kernel_b, block_width, skew_flipped)
        step_col = step_sizes[:, None]
        limit_col = (step_sizes * thresholds)[:, None]

        projected_wide = widened(projected, ghost)

        def shrink_step(iteration, carried):
            current, current_b = carried
            rebuilt = convolve_blocks(matrices, current_b, zero_rim, block_width)
            residual = (projected_wide - mix_atoms(rebuilt)) * inside[None, :]
            descent = correlate_blocks(flipped, residual.astype(jnp.bfloat16), zero_rim, block_width)
            stepped = current + step_col * descent
            shrunk = (
                allowed_wide[None, :]
                * jnp.sign(stepped)
                * jnp.maximum(jnp.abs(stepped) - limit_col, 0.0)
            )
            return (shrunk, shrunk.astype(jnp.bfloat16))

        for chunk in range(ITERS // CHUNK):
            wide = widened(latent, ghost)
            wide, _ = lax.fori_loop(0, CHUNK, shrink_step, (wide, wide.astype(jnp.bfloat16)))
            latent = wide[:, ghost : ghost + seg_len]
        rebuilt, before, latent_b = reconstruct(matrices, latent, block_width, tap_count)
        rebuilt_b = rebuilt.astype(jnp.bfloat16)
        row_part = jnp.dot(signal, rebuilt_b.T, preferred_element_type=jnp.float32)
        others = projected - jnp.dot(
            gram_matrix - jnp.diag(jnp.diag(gram_matrix)), rebuilt, precision=highest
        )
        code_ext = jnp.concatenate([before, latent_b], axis=1)
        taps_part = lag_sums(code_ext, others, block_width, tap_count)
        cross_part = jnp.dot(rebuilt, rebuilt.T, precision=highest)
        joined = butterfly_sum(jnp.concatenate([row_part, cross_part, taps_part.T], axis=0), "seg")
        stats_rows = joined[:chan_rows]
        cross_gram = joined[chan_rows : chan_rows + atoms_all]
        raw_kernel = joined[chan_rows + atoms_all :].T
        raw_rows = stats_rows - jnp.dot(
            space_loc, cross_gram - jnp.diag(jnp.diag(cross_gram)), precision=highest
        )
        raw_gram = butterfly_sum(jnp.dot(raw_rows.T, raw_rows, precision=highest), "chan")
        scaling = 1.0 / jnp.sqrt(jnp.diag(raw_gram) + epsilon)
        space_loc = raw_rows * scaling[None, :]
        gram_matrix = raw_gram * scaling[:, None] * scaling[None, :]
        kernel = raw_kernel / jnp.sqrt(
            jnp.sum(raw_kernel * raw_kernel, axis=1, keepdims=True) + epsilon
        )
    return (latent, space_loc, kernel)


def solution(mesh):
    placed = (P("chan", "seg"), P("chan", None), P(), P(None, "seg"), P(), P(), P())
    return jax.shard_map(
        on_device,
        mesh=mesh,
        in_specs=placed,
        out_specs=(P(None, "seg"), P("chan", None), P()),
        check_vma=False,
    )
```

```python
import jax
import jax.numpy as jnp
from jax import lax
from jax.sharding import PartitionSpec as P

ITERS = 10
OUTER = 2
CHUNK = 5
GHOST_BLOCKS = 20


epsilon = 1e-06
highest = lax.Precision.HIGHEST


def passed_along(value, axis, steps):
    count = lax.axis_size(axis)
    leading, last = (max(0, -steps), min(count, count - steps))
    return lax.ppermute(value, axis, [(source, source + steps) for source in range(leading, last)])


def widened(rows, ghost):
    seg_len = rows.shape[1]
    from_left = passed_along(rows[:, seg_len - ghost :], "seg", 1)
    from_right = passed_along(rows[:, :ghost], "seg", -1)
    return jnp.concatenate([from_left, rows, from_right], axis=1)


def butterfly_sum(value, axis):
    count = lax.axis_size(axis)
    distance = 1
    while distance < count:
        partner = lax.ppermute(value, axis, [(i, i ^ distance) for i in range(count)])
        value = value + partner
        distance *= 2
    return value


def one_hot_skew(block_width, tap_span, transposed=False):
    shape = (tap_span, block_width, block_width)
    d = lax.broadcasted_iota(jnp.int32, shape, 0)
    m = lax.broadcasted_iota(jnp.int32, shape, 2 if transposed else 1)
    i = lax.broadcasted_iota(jnp.int32, shape, 1 if transposed else 2)
    hit = d == i - m + (block_width - 1)
    return jnp.where(hit, 1.0, 0.0).astype(jnp.bfloat16).reshape(tap_span, block_width * block_width)


def band_sums_matrix(block_width, tap_count, offset):
    shape = (block_width, block_width, tap_count)
    m = lax.broadcasted_iota(jnp.int32, shape, 0)
    i = lax.broadcasted_iota(jnp.int32, shape, 1)
    tau = lax.broadcasted_iota(jnp.int32, shape, 2)
    hit = tau == i - m + block_width * offset
    return jnp.where(hit, 1.0, 0.0).reshape(block_width * block_width, tap_count)


def toeplitz(kernel_taps, block_width, skew):
    atoms_here, tap_count = kernel_taps.shape
    zero_pad = jnp.zeros((atoms_here, block_width), kernel_taps.dtype)
    padded = jnp.concatenate([zero_pad, kernel_taps, zero_pad, zero_pad], axis=1)
    lag_blocks = tap_count // block_width
    tap_span = 2 * block_width
    bands = jnp.concatenate(
        [padded[:, off * block_width + 1 : off * block_width + 1 + tap_span] for off in range(lag_blocks + 1)],
        axis=0,
    )
    flat = jnp.dot(bands, skew, preferred_element_type=jnp.float32).astype(kernel_taps.dtype)
    flat = flat.reshape(lag_blocks + 1, atoms_here, block_width, block_width)
    return [flat[off] for off in range(lag_blocks + 1)]


def lag_sums(code_ext, others, block_width, tap_count):
    atoms_here, seg_len = others.shape
    block_count = seg_len // block_width
    lag_blocks = tap_count // block_width
    extended = code_ext.reshape(atoms_here, block_count + lag_blocks, block_width)
    others_blocks = others.reshape(atoms_here, block_count, block_width)
    total = jnp.zeros((atoms_here, tap_count), jnp.float32)
    for offset in range(lag_blocks + 1):
        window = extended[:, lag_blocks - offset : lag_blocks - offset + block_count]
        grad = jnp.einsum(
            "kbm,kbi->kmi", window, others_blocks, preferred_element_type=jnp.float32, precision=highest
        ).reshape(atoms_here, block_width * block_width)
        total = total + jnp.dot(grad, band_sums_matrix(block_width, tap_count, offset), precision=highest)
    return total


def convolve_blocks(matrices, code_rows, before, block_width):
    atoms_here, seg_len = code_rows.shape
    block_count = seg_len // block_width
    lag_blocks = len(matrices) - 1
    extended = jnp.concatenate([before, code_rows], axis=1).reshape(
        atoms_here, block_count + lag_blocks, block_width
    )
    summed = jnp.zeros((atoms_here, block_count, block_width), jnp.float32)
    for offset, matrix in enumerate(matrices):
        window = extended[:, lag_blocks - offset : lag_blocks - offset + block_count]
        summed = summed + jnp.einsum(
            "kbm,kmi->kbi", window, matrix, preferred_element_type=jnp.float32, precision=highest
        )
    return summed.reshape(atoms_here, seg_len)


def correlate_blocks(matrices, residual_b, after_rim, block_width):
    atoms_here, seg_len = residual_b.shape
    block_count = seg_len // block_width
    extended = jnp.concatenate([residual_b, after_rim], axis=1).reshape(
        atoms_here, block_count + len(matrices) - 1, block_width
    )
    summed = jnp.zeros((atoms_here, block_count, block_width), jnp.float32)
    for offset, matrix in enumerate(matrices):
        window = extended[:, offset : offset + block_count]
        summed = summed + jnp.einsum(
            "kbi,kim->kbm", window, matrix, preferred_element_type=jnp.float32, precision=highest
        )
    return summed.reshape(atoms_here, seg_len)


def reconstruct(matrices, latent_rows, block_width, tap_count):
    latent_b = latent_rows.astype(jnp.bfloat16)
    before = passed_along(latent_b[:, latent_b.shape[1] - tap_count :], "seg", 1)
    return (convolve_blocks(matrices, latent_b, before, block_width), before, latent_b)


def on_device(signal, spatial, temporal, start_codes, thresholds, step_sizes, breaks):
    chan_rows, seg_len = signal.shape
    atoms_all, tap_count = temporal.shape
    block_width = 64
    skew = one_hot_skew(block_width, 2 * block_width)
    skew_flipped = one_hot_skew(block_width, 2 * block_width, transposed=True)
    ghost = GHOST_BLOCKS * block_width
    wide_positions = lax.axis_index("seg") * seg_len - ghost + lax.iota(jnp.int32, seg_len + 2 * ghost)
    wide_crosses = (wide_positions[None, :] < breaks[:, None]) & (
        breaks[:, None] < wide_positions[None, :] + tap_count
    )
    inside = jnp.where(
        (wide_positions >= 0) & (wide_positions < seg_len * lax.axis_size("seg")), 1.0, 0.0
    ).astype(jnp.float32)
    allowed_wide = inside * jnp.where(jnp.any(wide_crosses, axis=0), 0.0, 1.0).astype(jnp.float32)
    zero_rim = jnp.zeros((atoms_all, tap_count), jnp.bfloat16)
    raw_start = butterfly_sum(jnp.dot(spatial.T, spatial, precision=highest), "chan")
    scaling = 1.0 / jnp.sqrt(jnp.diag(raw_start) + epsilon)
    space_loc = spatial * scaling[None, :]
    gram_matrix = raw_start * scaling[:, None] * scaling[None, :]
    kernel = temporal / jnp.sqrt(jnp.sum(temporal * temporal, axis=1, keepdims=True) + epsilon)
    latent = start_codes
    for sweep_index in range(OUTER):
        space_b = space_loc.astype(jnp.bfloat16)
        kernel_b = kernel.astype(jnp.bfloat16)
        projected = butterfly_sum(
            jnp.dot(space_b.T, signal, preferred_element_type=jnp.float32), "chan"
        )
        own_gram = gram_matrix

        def mix_atoms(rebuilt_part):
            return jnp.dot(own_gram, rebuilt_part, precision=highest)

        matrices = toeplitz(kernel_b, block_width, skew)
        flipped = toeplitz(kernel_b, block_width, skew_flipped)
        step_col = step_sizes[:, None]
        limit_col = (step_sizes * thresholds)[:, None]

        projected_wide = widened(projected, ghost)

        def shrink_step(iteration, carried):
            current, current_b = carried
            rebuilt = convolve_blocks(matrices, current_b, zero_rim, block_width)
            residual = (projected_wide - mix_atoms(rebuilt)) * inside[None, :]
            descent = correlate_blocks(flipped, residual.astype(jnp.bfloat16), zero_rim, block_width)
            stepped = current + step_col * descent
            shrunk = (
                allowed_wide[None, :]
                * jnp.sign(stepped)
                * jnp.maximum(jnp.abs(stepped) - limit_col, 0.0)
            )
            return (shrunk, shrunk.astype(jnp.bfloat16))

        for chunk in range(ITERS // CHUNK):
            wide = widened(latent, ghost)
            wide, _ = lax.fori_loop(0, CHUNK, shrink_step, (wide, wide.astype(jnp.bfloat16)))
            latent = wide[:, ghost : ghost + seg_len]
        rebuilt, before, latent_b = reconstruct(matrices, latent, block_width, tap_count)
        rebuilt_b = rebuilt.astype(jnp.bfloat16)
        row_part = jnp.dot(signal, rebuilt_b.T, preferred_element_type=jnp.float32)
        others = projected - jnp.dot(
            gram_matrix - jnp.diag(jnp.diag(gram_matrix)), rebuilt, precision=highest
        )
        code_ext = jnp.concatenate([before, latent_b], axis=1)
        taps_part = lag_sums(code_ext, others, block_width, tap_count)
        cross_part = jnp.dot(rebuilt, rebuilt.T, precision=highest)
        joined = butterfly_sum(jnp.concatenate([row_part, cross_part, taps_part.T], axis=0), "seg")
        stats_rows = joined[:chan_rows]
        cross_gram = joined[chan_rows : chan_rows + atoms_all]
        raw_kernel = joined[chan_rows + atoms_all :].T
        raw_rows = stats_rows - jnp.dot(
            space_loc, cross_gram - jnp.diag(jnp.diag(cross_gram)), precision=highest
        )
        raw_gram = butterfly_sum(jnp.dot(raw_rows.T, raw_rows, precision=highest), "chan")
        scaling = 1.0 / jnp.sqrt(jnp.diag(raw_gram) + epsilon)
        space_loc = raw_rows * scaling[None, :]
        gram_matrix = raw_gram * scaling[:, None] * scaling[None, :]
        kernel = raw_kernel / jnp.sqrt(
            jnp.sum(raw_kernel * raw_kernel, axis=1, keepdims=True) + epsilon
        )
    return (latent, space_loc, kernel)


def solution(mesh):
    placed = (P("chan", "seg"), P("chan", None), P(), P(None, "seg"), P(), P(), P())
    return jax.shard_map(
        on_device,
        mesh=mesh,
        in_specs=placed,
        out_specs=(P(None, "seg"), P("chan", None), P()),
        check_vma=False,
    )
```

```python
import jax
import jax.numpy as jnp
from jax import lax
from jax.sharding import PartitionSpec as P

ITERS = 10
OUTER = 2
CHUNK = 5
GHOST_BLOCKS = 10


epsilon = 1e-06
highest = lax.Precision.HIGHEST


def passed_along(value, axis, steps):
    count = lax.axis_size(axis)
    leading, last = (max(0, -steps), min(count, count - steps))
    return lax.ppermute(value, axis, [(source, source + steps) for source in range(leading, last)])


def widened(rows, ghost):
    seg_len = rows.shape[1]
    from_left = passed_along(rows[:, seg_len - ghost :], "seg", 1)
    from_right = passed_along(rows[:, :ghost], "seg", -1)
    return jnp.concatenate([from_left, rows, from_right], axis=1)


def butterfly_sum(value, axis):
    count = lax.axis_size(axis)
    distance = 1
    while distance < count:
        partner = lax.ppermute(value, axis, [(i, i ^ distance) for i in range(count)])
        value = value + partner
        distance *= 2
    return value


def one_hot_skew(block_width, tap_span, transposed=False):
    shape = (tap_span, block_width, block_width)
    d = lax.broadcasted_iota(jnp.int32, shape, 0)
    m = lax.broadcasted_iota(jnp.int32, shape, 2 if transposed else 1)
    i = lax.broadcasted_iota(jnp.int32, shape, 1 if transposed else 2)
    hit = d == i - m + (block_width - 1)
    return jnp.where(hit, 1.0, 0.0).astype(jnp.bfloat16).reshape(tap_span, block_width * block_width)


def band_sums_matrix(block_width, tap_count, offset):
    shape = (block_width, block_width, tap_count)
    m = lax.broadcasted_iota(jnp.int32, shape, 0)
    i = lax.broadcasted_iota(jnp.int32, shape, 1)
    tau = lax.broadcasted_iota(jnp.int32, shape, 2)
    hit = tau == i - m + block_width * offset
    return jnp.where(hit, 1.0, 0.0).reshape(block_width * block_width, tap_count)


def toeplitz(kernel_taps, block_width, skew):
    atoms_here, tap_count = kernel_taps.shape
    zero_pad = jnp.zeros((atoms_here, block_width), kernel_taps.dtype)
    padded = jnp.concatenate([zero_pad, kernel_taps, zero_pad, zero_pad], axis=1)
    lag_blocks = tap_count // block_width
    tap_span = 2 * block_width
    bands = jnp.concatenate(
        [padded[:, off * block_width + 1 : off * block_width + 1 + tap_span] for off in range(lag_blocks + 1)],
        axis=0,
    )
    flat = jnp.dot(bands, skew, preferred_element_type=jnp.float32).astype(kernel_taps.dtype)
    flat = flat.reshape(lag_blocks + 1, atoms_here, block_width, block_width)
    return [flat[off] for off in range(lag_blocks + 1)]


def lag_sums(code_ext, others, block_width, tap_count):
    atoms_here, seg_len = others.shape
    block_count = seg_len // block_width
    lag_blocks = tap_count // block_width
    extended = code_ext.reshape(atoms_here, block_count + lag_blocks, block_width)
    others_blocks = others.reshape(atoms_here, block_count, block_width)
    total = jnp.zeros((atoms_here, tap_count), jnp.float32)
    for offset in range(lag_blocks + 1):
        window = extended[:, lag_blocks - offset : lag_blocks - offset + block_count]
        grad = jnp.einsum(
            "kbm,kbi->kmi", window, others_blocks, preferred_element_type=jnp.float32, precision=highest
        ).reshape(atoms_here, block_width * block_width)
        total = total + jnp.dot(grad, band_sums_matrix(block_width, tap_count, offset), precision=highest)
    return total


def convolve_blocks(matrices, code_rows, before, block_width):
    atoms_here, seg_len = code_rows.shape
    block_count = seg_len // block_width
    lag_blocks = len(matrices) - 1
    extended = jnp.concatenate([before, code_rows], axis=1).reshape(
        atoms_here, block_count + lag_blocks, block_width
    )
    summed = jnp.zeros((atoms_here, block_count, block_width), jnp.float32)
    for offset, matrix in enumerate(matrices):
        window = extended[:, lag_blocks - offset : lag_blocks - offset + block_count]
        summed = summed + jnp.einsum(
            "kbm,kmi->kbi", window, matrix, preferred_element_type=jnp.float32, precision=highest
        )
    return summed.reshape(atoms_here, seg_len)


def correlate_blocks(matrices, residual_b, after_rim, block_width):
    atoms_here, seg_len = residual_b.shape
    block_count = seg_len // block_width
    extended = jnp.concatenate([residual_b, after_rim], axis=1).reshape(
        atoms_here, block_count + len(matrices) - 1, block_width
    )
    summed = jnp.zeros((atoms_here, block_count, block_width), jnp.float32)
    for offset, matrix in enumerate(matrices):
        window = extended[:, offset : offset + block_count]
        summed = summed + jnp.einsum(
            "kbi,kim->kbm", window, matrix, preferred_element_type=jnp.float32, precision=highest
        )
    return summed.reshape(atoms_here, seg_len)


def reconstruct(matrices, latent_rows, block_width, tap_count):
    latent_b = latent_rows.astype(jnp.bfloat16)
    before = passed_along(latent_b[:, latent_b.shape[1] - tap_count :], "seg", 1)
    return (convolve_blocks(matrices, latent_b, before, block_width), before, latent_b)


def on_device(signal, spatial, temporal, start_codes, thresholds, step_sizes, breaks):
    chan_rows, seg_len = signal.shape
    atoms_all, tap_count = temporal.shape
    block_width = 128
    skew = one_hot_skew(block_width, 2 * block_width)
    skew_flipped = one_hot_skew(block_width, 2 * block_width, transposed=True)
    ghost = GHOST_BLOCKS * block_width
    wide_positions = lax.axis_index("seg") * seg_len - ghost + lax.iota(jnp.int32, seg_len + 2 * ghost)
    wide_crosses = (wide_positions[None, :] < breaks[:, None]) & (
        breaks[:, None] < wide_positions[None, :] + tap_count
    )
    inside = jnp.where(
        (wide_positions >= 0) & (wide_positions < seg_len * lax.axis_size("seg")), 1.0, 0.0
    ).astype(jnp.float32)
    allowed_wide = inside * jnp.where(jnp.any(wide_crosses, axis=0), 0.0, 1.0).astype(jnp.float32)
    zero_rim = jnp.zeros((atoms_all, tap_count), jnp.bfloat16)
    raw_start = butterfly_sum(jnp.dot(spatial.T, spatial, precision=highest), "chan")
    scaling = 1.0 / jnp.sqrt(jnp.diag(raw_start) + epsilon)
    space_loc = spatial * scaling[None, :]
    gram_matrix = raw_start * scaling[:, None] * scaling[None, :]
    kernel = temporal / jnp.sqrt(jnp.sum(temporal * temporal, axis=1, keepdims=True) + epsilon)
    latent = start_codes
    for sweep_index in range(OUTER):
        space_b = space_loc.astype(jnp.bfloat16)
        kernel_b = kernel.astype(jnp.bfloat16)
        projected = butterfly_sum(
            jnp.dot(space_b.T, signal, preferred_element_type=jnp.float32), "chan"
        )
        own_gram = gram_matrix

        def mix_atoms(rebuilt_part):
            return jnp.dot(own_gram, rebuilt_part, precision=highest)

        matrices = toeplitz(kernel_b, block_width, skew)
        flipped = toeplitz(kernel_b, block_width, skew_flipped)
        step_col = step_sizes[:, None]
        limit_col = (step_sizes * thresholds)[:, None]

        projected_wide = widened(projected, ghost)

        def shrink_step(iteration, carried):
            current, current_b = carried
            rebuilt = convolve_blocks(matrices, current_b, zero_rim, block_width)
            residual = (projected_wide - mix_atoms(rebuilt)) * inside[None, :]
            descent = correlate_blocks(flipped, residual.astype(jnp.bfloat16), zero_rim, block_width)
            stepped = current + step_col * descent
            shrunk = (
                allowed_wide[None, :]
                * jnp.sign(stepped)
                * jnp.maximum(jnp.abs(stepped) - limit_col, 0.0)
            )
            return (shrunk, shrunk.astype(jnp.bfloat16))

        for chunk in range(ITERS // CHUNK):
            wide = widened(latent, ghost)
            wide, _ = lax.fori_loop(0, CHUNK, shrink_step, (wide, wide.astype(jnp.bfloat16)))
            latent = wide[:, ghost : ghost + seg_len]
        rebuilt, before, latent_b = reconstruct(matrices, latent, block_width, tap_count)
        rebuilt_b = rebuilt.astype(jnp.bfloat16)
        row_part = jnp.dot(rebuilt_b, signal.T, preferred_element_type=jnp.float32)
        others = projected - jnp.dot(
            gram_matrix - jnp.diag(jnp.diag(gram_matrix)), rebuilt, precision=highest
        )
        code_ext = jnp.concatenate([before, latent_b], axis=1)
        taps_part = lag_sums(code_ext, others, block_width, tap_count)
        cross_part = jnp.dot(rebuilt, rebuilt.T, precision=highest)
        joined = butterfly_sum(jnp.concatenate([row_part, cross_part, taps_part], axis=1), "seg")
        stats_rows = joined[:, :chan_rows].T
        cross_gram = joined[:, chan_rows : chan_rows + atoms_all]
        raw_kernel = joined[:, chan_rows + atoms_all :]
        raw_rows = stats_rows - jnp.dot(
            space_loc, cross_gram - jnp.diag(jnp.diag(cross_gram)), precision=highest
        )
        raw_gram = butterfly_sum(jnp.dot(raw_rows.T, raw_rows, precision=highest), "chan")
        scaling = 1.0 / jnp.sqrt(jnp.diag(raw_gram) + epsilon)
        space_loc = raw_rows * scaling[None, :]
        gram_matrix = raw_gram * scaling[:, None] * scaling[None, :]
        kernel = raw_kernel / jnp.sqrt(
            jnp.sum(raw_kernel * raw_kernel, axis=1, keepdims=True) + epsilon
        )
    return (latent, space_loc, kernel)


def solution(mesh):
    placed = (P("chan", "seg"), P("chan", None), P(), P(None, "seg"), P(), P(), P())
    return jax.shard_map(
        on_device,
        mesh=mesh,
        in_specs=placed,
        out_specs=(P(None, "seg"), P("chan", None), P()),
        check_vma=False,
    )
```

```python
import jax
import jax.numpy as jnp
from jax import lax
from jax.sharding import PartitionSpec as P

ITERS = 10
OUTER = 2
CHUNK = 5
GHOST_BLOCKS = 10


epsilon = 1e-06
highest = lax.Precision.HIGHEST


def passed_along(value, axis, steps):
    count = lax.axis_size(axis)
    leading, last = (max(0, -steps), min(count, count - steps))
    return lax.ppermute(value, axis, [(source, source + steps) for source in range(leading, last)])


def widened(rows, ghost):
    seg_len = rows.shape[1]
    from_left = passed_along(rows[:, seg_len - ghost :], "seg", 1)
    from_right = passed_along(rows[:, :ghost], "seg", -1)
    return jnp.concatenate([from_left, rows, from_right], axis=1)


def butterfly_sum(value, axis):
    count = lax.axis_size(axis)
    distance = 1
    while distance < count:
        partner = lax.ppermute(value, axis, [(i, i ^ distance) for i in range(count)])
        value = value + partner
        distance *= 2
    return value


def halving_sum(value, axis):
    count = lax.axis_size(axis)
    me = lax.axis_index(axis)
    distances = []
    distance = 1
    while distance < count:
        distances.append(distance)
        distance *= 2
    kept = value
    for distance in distances:
        half = kept.shape[1] // 2
        lower, upper = kept[:, :half], kept[:, half:]
        upper_here = (me // distance) % 2 == 1
        keep = jnp.where(upper_here, upper, lower)
        send = jnp.where(upper_here, lower, upper)
        kept = keep + lax.ppermute(send, axis, [(i, i ^ distance) for i in range(count)])
    for distance in reversed(distances):
        other = lax.ppermute(kept, axis, [(i, i ^ distance) for i in range(count)])
        upper_here = (me // distance) % 2 == 1
        kept = jnp.where(
            upper_here,
            jnp.concatenate([other, kept], axis=1),
            jnp.concatenate([kept, other], axis=1),
        )
    return kept


def one_hot_skew(block_width, tap_span, transposed=False):
    shape = (tap_span, block_width, block_width)
    d = lax.broadcasted_iota(jnp.int32, shape, 0)
    m = lax.broadcasted_iota(jnp.int32, shape, 2 if transposed else 1)
    i = lax.broadcasted_iota(jnp.int32, shape, 1 if transposed else 2)
    hit = d == i - m + (block_width - 1)
    return jnp.where(hit, 1.0, 0.0).astype(jnp.bfloat16).reshape(tap_span, block_width * block_width)


def band_sums_matrix(block_width, tap_count, offset):
    shape = (block_width, block_width, tap_count)
    m = lax.broadcasted_iota(jnp.int32, shape, 0)
    i = lax.broadcasted_iota(jnp.int32, shape, 1)
    tau = lax.broadcasted_iota(jnp.int32, shape, 2)
    hit = tau == i - m + block_width * offset
    return jnp.where(hit, 1.0, 0.0).reshape(block_width * block_width, tap_count)


def toeplitz(kernel_taps, block_width, skew):
    atoms_here, tap_count = kernel_taps.shape
    zero_pad = jnp.zeros((atoms_here, block_width), kernel_taps.dtype)
    padded = jnp.concatenate([zero_pad, kernel_taps, zero_pad, zero_pad], axis=1)
    lag_blocks = tap_count // block_width
    tap_span = 2 * block_width
    bands = jnp.concatenate(
        [padded[:, off * block_width + 1 : off * block_width + 1 + tap_span] for off in range(lag_blocks + 1)],
        axis=0,
    )
    flat = jnp.dot(bands, skew, preferred_element_type=jnp.float32).astype(kernel_taps.dtype)
    flat = flat.reshape(lag_blocks + 1, atoms_here, block_width, block_width)
    return [flat[off] for off in range(lag_blocks + 1)]


def lag_sums(code_ext, others, block_width, tap_count):
    atoms_here, seg_len = others.shape
    block_count = seg_len // block_width
    lag_blocks = tap_count // block_width
    extended = code_ext.reshape(atoms_here, block_count + lag_blocks, block_width)
    others_blocks = others.reshape(atoms_here, block_count, block_width)
    total = jnp.zeros((atoms_here, tap_count), jnp.float32)
    for offset in range(lag_blocks + 1):
        window = extended[:, lag_blocks - offset : lag_blocks - offset + block_count]
        grad = jnp.einsum(
            "kbm,kbi->kmi", window, others_blocks, preferred_element_type=jnp.float32, precision=highest
        ).reshape(atoms_here, block_width * block_width)
        total = total + jnp.dot(grad, band_sums_matrix(block_width, tap_count, offset), precision=highest)
    return total


def convolve_blocks(matrices, code_rows, before, block_width):
    atoms_here, seg_len = code_rows.shape
    block_count = seg_len // block_width
    lag_blocks = len(matrices) - 1
    extended = jnp.concatenate([before, code_rows], axis=1).reshape(
        atoms_here, block_count + lag_blocks, block_width
    )
    summed = jnp.zeros((atoms_here, block_count, block_width), jnp.float32)
    for offset, matrix in enumerate(matrices):
        window = extended[:, lag_blocks - offset : lag_blocks - offset + block_count]
        summed = summed + jnp.einsum(
            "kbm,kmi->kbi", window, matrix, preferred_element_type=jnp.float32, precision=highest
        )
    return summed.reshape(atoms_here, seg_len)


def correlate_blocks(matrices, residual_b, after_rim, block_width):
    atoms_here, seg_len = residual_b.shape
    block_count = seg_len // block_width
    extended = jnp.concatenate([residual_b, after_rim], axis=1).reshape(
        atoms_here, block_count + len(matrices) - 1, block_width
    )
    summed = jnp.zeros((atoms_here, block_count, block_width), jnp.float32)
    for offset, matrix in enumerate(matrices):
        window = extended[:, offset : offset + block_count]
        summed = summed + jnp.einsum(
            "kbi,kim->kbm", window, matrix, preferred_element_type=jnp.float32, precision=highest
        )
    return summed.reshape(atoms_here, seg_len)


def reconstruct(matrices, latent_rows, block_width, tap_count):
    latent_b = latent_rows.astype(jnp.bfloat16)
    before = passed_along(latent_b[:, latent_b.shape[1] - tap_count :], "seg", 1)
    return (convolve_blocks(matrices, latent_b, before, block_width), before, latent_b)


def on_device(signal, spatial, temporal, start_codes, thresholds, step_sizes, breaks):
    chan_rows, seg_len = signal.shape
    atoms_all, tap_count = temporal.shape
    block_width = 128
    skew = one_hot_skew(block_width, 2 * block_width)
    skew_flipped = one_hot_skew(block_width, 2 * block_width, transposed=True)
    ghost = GHOST_BLOCKS * block_width
    wide_positions = lax.axis_index("seg") * seg_len - ghost + lax.iota(jnp.int32, seg_len + 2 * ghost)
    wide_crosses = (wide_positions[None, :] < breaks[:, None]) & (
        breaks[:, None] < wide_positions[None, :] + tap_count
    )
    inside = jnp.where(
        (wide_positions >= 0) & (wide_positions < seg_len * lax.axis_size("seg")), 1.0, 0.0
    ).astype(jnp.float32)
    allowed_wide = inside * jnp.where(jnp.any(wide_crosses, axis=0), 0.0, 1.0).astype(jnp.float32)
    zero_rim = jnp.zeros((atoms_all, tap_count), jnp.bfloat16)
    raw_start = butterfly_sum(jnp.dot(spatial.T, spatial, precision=highest), "chan")
    scaling = 1.0 / jnp.sqrt(jnp.diag(raw_start) + epsilon)
    space_loc = spatial * scaling[None, :]
    gram_matrix = raw_start * scaling[:, None] * scaling[None, :]
    kernel = temporal / jnp.sqrt(jnp.sum(temporal * temporal, axis=1, keepdims=True) + epsilon)
    latent = start_codes
    for sweep_index in range(OUTER):
        space_b = space_loc.astype(jnp.bfloat16)
        kernel_b = kernel.astype(jnp.bfloat16)
        projected = halving_sum(
            jnp.dot(space_b.T, signal, preferred_element_type=jnp.float32), "chan"
        )
        own_gram = gram_matrix

        def mix_atoms(rebuilt_part):
            return jnp.dot(own_gram, rebuilt_part, precision=highest)

        matrices = toeplitz(kernel_b, block_width, skew)
        flipped = toeplitz(kernel_b, block_width, skew_flipped)
        step_col = step_sizes[:, None]
        limit_col = (step_sizes * thresholds)[:, None]

        projected_wide = widened(projected, ghost)

        def shrink_step(iteration, carried):
            current, current_b = carried
            rebuilt = convolve_blocks(matrices, current_b, zero_rim, block_width)
            residual = (projected_wide - mix_atoms(rebuilt)) * inside[None, :]
            descent = correlate_blocks(flipped, residual.astype(jnp.bfloat16), zero_rim, block_width)
            stepped = current + step_col * descent
            shrunk = (
                allowed_wide[None, :]
                * jnp.sign(stepped)
                * jnp.maximum(jnp.abs(stepped) - limit_col, 0.0)
            )
            return (shrunk, shrunk.astype(jnp.bfloat16))

        for chunk in range(ITERS // CHUNK):
            wide = widened(latent, ghost)
            wide, _ = lax.fori_loop(0, CHUNK, shrink_step, (wide, wide.astype(jnp.bfloat16)))
            latent = wide[:, ghost : ghost + seg_len]
        rebuilt, before, latent_b = reconstruct(matrices, latent, block_width, tap_count)
        rebuilt_b = rebuilt.astype(jnp.bfloat16)
        row_part = jnp.dot(rebuilt_b, signal.T, preferred_element_type=jnp.float32)
        others = projected - jnp.dot(
            gram_matrix - jnp.diag(jnp.diag(gram_matrix)), rebuilt, precision=highest
        )
        code_ext = jnp.concatenate([before, latent_b], axis=1)
        taps_part = lag_sums(code_ext, others, block_width, tap_count)
        cross_part = jnp.dot(rebuilt, rebuilt.T, precision=highest)
        joined = butterfly_sum(jnp.concatenate([row_part, cross_part, taps_part], axis=1), "seg")
        stats_rows = joined[:, :chan_rows].T
        cross_gram = joined[:, chan_rows : chan_rows + atoms_all]
        raw_kernel = joined[:, chan_rows + atoms_all :]
        raw_rows = stats_rows - jnp.dot(
            space_loc, cross_gram - jnp.diag(jnp.diag(cross_gram)), precision=highest
        )
        raw_gram = butterfly_sum(jnp.dot(raw_rows.T, raw_rows, precision=highest), "chan")
        scaling = 1.0 / jnp.sqrt(jnp.diag(raw_gram) + epsilon)
        space_loc = raw_rows * scaling[None, :]
        gram_matrix = raw_gram * scaling[:, None] * scaling[None, :]
        kernel = raw_kernel / jnp.sqrt(
            jnp.sum(raw_kernel * raw_kernel, axis=1, keepdims=True) + epsilon
        )
    return (latent, space_loc, kernel)


def solution(mesh):
    placed = (P("chan", "seg"), P("chan", None), P(), P(None, "seg"), P(), P(), P())
    return jax.shard_map(
        on_device,
        mesh=mesh,
        in_specs=placed,
        out_specs=(P(None, "seg"), P("chan", None), P()),
        check_vma=False,
    )
```

```python
import jax
import jax.numpy as jnp
from jax import lax
from jax.sharding import PartitionSpec as P

ITERS = 10
OUTER = 2
CHUNK = 5
GHOST_BLOCKS = 10


epsilon = 1e-06
highest = lax.Precision.HIGHEST


def passed_along(value, axis, steps):
    count = lax.axis_size(axis)
    leading, last = (max(0, -steps), min(count, count - steps))
    return lax.ppermute(value, axis, [(source, source + steps) for source in range(leading, last)])


def widened(rows, ghost):
    seg_len = rows.shape[1]
    from_left = passed_along(rows[:, seg_len - ghost :], "seg", 1)
    from_right = passed_along(rows[:, :ghost], "seg", -1)
    return jnp.concatenate([from_left, rows, from_right], axis=1)


def butterfly_sum(value, axis):
    count = lax.axis_size(axis)
    distance = 1
    while distance < count:
        partner = lax.ppermute(value, axis, [(i, i ^ distance) for i in range(count)])
        value = value + partner
        distance *= 2
    return value


def one_hot_skew(block_width, tap_span, transposed=False):
    shape = (tap_span, block_width, block_width)
    d = lax.broadcasted_iota(jnp.int32, shape, 0)
    m = lax.broadcasted_iota(jnp.int32, shape, 2 if transposed else 1)
    i = lax.broadcasted_iota(jnp.int32, shape, 1 if transposed else 2)
    hit = d == i - m + (block_width - 1)
    return jnp.where(hit, 1.0, 0.0).astype(jnp.bfloat16).reshape(tap_span, block_width * block_width)


def band_sums_matrix(block_width, first_lag, lag_count, offset):
    shape = (block_width, block_width, lag_count)
    m = lax.broadcasted_iota(jnp.int32, shape, 0)
    i = lax.broadcasted_iota(jnp.int32, shape, 1)
    tau = lax.broadcasted_iota(jnp.int32, shape, 2) + first_lag
    hit = tau == i - m + block_width * offset
    return jnp.where(hit, 1.0, 0.0).reshape(block_width * block_width, lag_count)


def toeplitz(kernel_taps, block_width, skew):
    atoms_here, tap_count = kernel_taps.shape
    zero_pad = jnp.zeros((atoms_here, block_width), kernel_taps.dtype)
    padded = jnp.concatenate([zero_pad, kernel_taps, zero_pad, zero_pad], axis=1)
    lag_blocks = tap_count // block_width
    tap_span = 2 * block_width
    bands = jnp.concatenate(
        [padded[:, off * block_width + 1 : off * block_width + 1 + tap_span] for off in range(lag_blocks + 1)],
        axis=0,
    )
    flat = jnp.dot(bands, skew, preferred_element_type=jnp.float32).astype(kernel_taps.dtype)
    flat = flat.reshape(lag_blocks + 1, atoms_here, block_width, block_width)
    return [flat[off] for off in range(lag_blocks + 1)]


def lag_sums(code_ext, others, block_width, tap_count):
    atoms_here, seg_len = others.shape
    block_count = seg_len // block_width
    lag_blocks = tap_count // block_width
    extended = code_ext.reshape(atoms_here, block_count + lag_blocks, block_width)
    others_blocks = others.reshape(atoms_here, block_count, block_width)
    total = jnp.zeros((atoms_here, tap_count), jnp.float32)
    for offset in range(lag_blocks + 1):
        window = extended[:, lag_blocks - offset : lag_blocks - offset + block_count]
        grad = jnp.einsum(
            "kbm,kbi->kmi", window, others_blocks, preferred_element_type=jnp.float32, precision=highest
        ).reshape(atoms_here, block_width * block_width)
        first_lag = max(0, block_width * (offset - 1) + 1)
        last_lag = min(tap_count, block_width * (offset + 1))
        first_lag = (first_lag // block_width) * block_width
        lag_count = ((last_lag - first_lag + block_width - 1) // block_width) * block_width
        part = jnp.dot(grad, band_sums_matrix(block_width, first_lag, lag_count, offset), precision=highest)
        total = total.at[:, first_lag : first_lag + lag_count].add(part)
    return total


def convolve_blocks(matrices, code_rows, before, block_width):
    atoms_here, seg_len = code_rows.shape
    block_count = seg_len // block_width
    lag_blocks = len(matrices) - 1
    extended = jnp.concatenate([before, code_rows], axis=1).reshape(
        atoms_here, block_count + lag_blocks, block_width
    )
    summed = jnp.zeros((atoms_here, block_count, block_width), jnp.float32)
    for offset, matrix in enumerate(matrices):
        window = extended[:, lag_blocks - offset : lag_blocks - offset + block_count]
        summed = summed + jnp.einsum(
            "kbm,kmi->kbi", window, matrix, preferred_element_type=jnp.float32, precision=highest
        )
    return summed.reshape(atoms_here, seg_len)


def correlate_blocks(matrices, residual_b, after_rim, block_width):
    atoms_here, seg_len = residual_b.shape
    block_count = seg_len // block_width
    extended = jnp.concatenate([residual_b, after_rim], axis=1).reshape(
        atoms_here, block_count + len(matrices) - 1, block_width
    )
    summed = jnp.zeros((atoms_here, block_count, block_width), jnp.float32)
    for offset, matrix in enumerate(matrices):
        window = extended[:, offset : offset + block_count]
        summed = summed + jnp.einsum(
            "kbi,kim->kbm", window, matrix, preferred_element_type=jnp.float32, precision=highest
        )
    return summed.reshape(atoms_here, seg_len)


def reconstruct(matrices, latent_rows, block_width, tap_count):
    latent_b = latent_rows.astype(jnp.bfloat16)
    before = passed_along(latent_b[:, latent_b.shape[1] - tap_count :], "seg", 1)
    return (convolve_blocks(matrices, latent_b, before, block_width), before, latent_b)


def on_device(signal, spatial, temporal, start_codes, thresholds, step_sizes, breaks):
    chan_rows, seg_len = signal.shape
    atoms_all, tap_count = temporal.shape
    block_width = 128
    skew = one_hot_skew(block_width, 2 * block_width)
    skew_flipped = one_hot_skew(block_width, 2 * block_width, transposed=True)
    ghost = GHOST_BLOCKS * block_width
    wide_positions = lax.axis_index("seg") * seg_len - ghost + lax.iota(jnp.int32, seg_len + 2 * ghost)
    wide_crosses = (wide_positions[None, :] < breaks[:, None]) & (
        breaks[:, None] < wide_positions[None, :] + tap_count
    )
    inside = jnp.where(
        (wide_positions >= 0) & (wide_positions < seg_len * lax.axis_size("seg")), 1.0, 0.0
    ).astype(jnp.float32)
    allowed_wide = inside * jnp.where(jnp.any(wide_crosses, axis=0), 0.0, 1.0).astype(jnp.float32)
    zero_rim = jnp.zeros((atoms_all, tap_count), jnp.bfloat16)
    raw_start = butterfly_sum(jnp.dot(spatial.T, spatial, precision=highest), "chan")
    scaling = 1.0 / jnp.sqrt(jnp.diag(raw_start) + epsilon)
    space_loc = spatial * scaling[None, :]
    gram_matrix = raw_start * scaling[:, None] * scaling[None, :]
    kernel = temporal / jnp.sqrt(jnp.sum(temporal * temporal, axis=1, keepdims=True) + epsilon)
    latent = start_codes
    for sweep_index in range(OUTER):
        space_b = space_loc.astype(jnp.bfloat16)
        kernel_b = kernel.astype(jnp.bfloat16)
        projected = butterfly_sum(
            jnp.dot(space_b.T, signal, preferred_element_type=jnp.float32), "chan"
        )
        own_gram = gram_matrix

        def mix_atoms(rebuilt_part):
            return jnp.dot(own_gram, rebuilt_part, precision=highest)

        matrices = toeplitz(kernel_b, block_width, skew)
        flipped = toeplitz(kernel_b, block_width, skew_flipped)
        step_col = step_sizes[:, None]
        limit_col = (step_sizes * thresholds)[:, None]

        projected_wide = widened(projected, ghost)

        def shrink_step(iteration, carried):
            current, current_b = carried
            rebuilt = convolve_blocks(matrices, current_b, zero_rim, block_width)
            residual = (projected_wide - mix_atoms(rebuilt)) * inside[None, :]
            descent = correlate_blocks(flipped, residual.astype(jnp.bfloat16), zero_rim, block_width)
            stepped = current + step_col * descent
            shrunk = (
                allowed_wide[None, :]
                * jnp.sign(stepped)
                * jnp.maximum(jnp.abs(stepped) - limit_col, 0.0)
            )
            return (shrunk, shrunk.astype(jnp.bfloat16))

        for chunk in range(ITERS // CHUNK):
            wide = widened(latent, ghost)
            wide, _ = lax.fori_loop(0, CHUNK, shrink_step, (wide, wide.astype(jnp.bfloat16)))
            latent = wide[:, ghost : ghost + seg_len]
        rebuilt, before, latent_b = reconstruct(matrices, latent, block_width, tap_count)
        rebuilt_b = rebuilt.astype(jnp.bfloat16)
        row_part = jnp.dot(rebuilt_b, signal.T, preferred_element_type=jnp.float32)
        others = projected - jnp.dot(
            gram_matrix - jnp.diag(jnp.diag(gram_matrix)), rebuilt, precision=highest
        )
        code_ext = jnp.concatenate([before, latent_b], axis=1)
        taps_part = lag_sums(code_ext, others, block_width, tap_count)
        cross_part = jnp.dot(rebuilt, rebuilt.T, precision=highest)
        joined = butterfly_sum(jnp.concatenate([row_part, cross_part, taps_part], axis=1), "seg")
        stats_rows = joined[:, :chan_rows].T
        cross_gram = joined[:, chan_rows : chan_rows + atoms_all]
        raw_kernel = joined[:, chan_rows + atoms_all :]
        raw_rows = stats_rows - jnp.dot(
            space_loc, cross_gram - jnp.diag(jnp.diag(cross_gram)), precision=highest
        )
        raw_gram = butterfly_sum(jnp.dot(raw_rows.T, raw_rows, precision=highest), "chan")
        scaling = 1.0 / jnp.sqrt(jnp.diag(raw_gram) + epsilon)
        space_loc = raw_rows * scaling[None, :]
        gram_matrix = raw_gram * scaling[:, None] * scaling[None, :]
        kernel = raw_kernel / jnp.sqrt(
            jnp.sum(raw_kernel * raw_kernel, axis=1, keepdims=True) + epsilon
        )
    return (latent, space_loc, kernel)


def solution(mesh):
    placed = (P("chan", "seg"), P("chan", None), P(), P(None, "seg"), P(), P(), P())
    return jax.shard_map(
        on_device,
        mesh=mesh,
        in_specs=placed,
        out_specs=(P(None, "seg"), P("chan", None), P()),
        check_vma=False,
    )
```

```python
import jax
import jax.numpy as jnp
from jax import lax
from jax.sharding import PartitionSpec as P

ITERS = 10
OUTER = 2
CHUNK = 5
GHOST_BLOCKS = 10
WIDE_STEPS = 3
NARROW_BLOCKS = 4


epsilon = 1e-06
highest = lax.Precision.HIGHEST


def passed_along(value, axis, steps):
    count = lax.axis_size(axis)
    leading, last = (max(0, -steps), min(count, count - steps))
    return lax.ppermute(value, axis, [(source, source + steps) for source in range(leading, last)])


def widened(rows, ghost):
    seg_len = rows.shape[1]
    from_left = passed_along(rows[:, seg_len - ghost :], "seg", 1)
    from_right = passed_along(rows[:, :ghost], "seg", -1)
    return jnp.concatenate([from_left, rows, from_right], axis=1)


def butterfly_sum(value, axis):
    count = lax.axis_size(axis)
    distance = 1
    while distance < count:
        partner = lax.ppermute(value, axis, [(i, i ^ distance) for i in range(count)])
        value = value + partner
        distance *= 2
    return value


def one_hot_skew(block_width, tap_span, transposed=False):
    shape = (tap_span, block_width, block_width)
    d = lax.broadcasted_iota(jnp.int32, shape, 0)
    m = lax.broadcasted_iota(jnp.int32, shape, 2 if transposed else 1)
    i = lax.broadcasted_iota(jnp.int32, shape, 1 if transposed else 2)
    hit = d == i - m + (block_width - 1)
    return jnp.where(hit, 1.0, 0.0).astype(jnp.bfloat16).reshape(tap_span, block_width * block_width)


def band_sums_matrix(block_width, tap_count, offset):
    shape = (block_width, block_width, tap_count)
    m = lax.broadcasted_iota(jnp.int32, shape, 0)
    i = lax.broadcasted_iota(jnp.int32, shape, 1)
    tau = lax.broadcasted_iota(jnp.int32, shape, 2)
    hit = tau == i - m + block_width * offset
    return jnp.where(hit, 1.0, 0.0).reshape(block_width * block_width, tap_count)


def toeplitz(kernel_taps, block_width, skew):
    atoms_here, tap_count = kernel_taps.shape
    zero_pad = jnp.zeros((atoms_here, block_width), kernel_taps.dtype)
    padded = jnp.concatenate([zero_pad, kernel_taps, zero_pad, zero_pad], axis=1)
    lag_blocks = tap_count // block_width
    tap_span = 2 * block_width
    bands = jnp.concatenate(
        [padded[:, off * block_width + 1 : off * block_width + 1 + tap_span] for off in range(lag_blocks + 1)],
        axis=0,
    )
    flat = jnp.dot(bands, skew, preferred_element_type=jnp.float32).astype(kernel_taps.dtype)
    flat = flat.reshape(lag_blocks + 1, atoms_here, block_width, block_width)
    return [flat[off] for off in range(lag_blocks + 1)]


def lag_sums(code_ext, others, block_width, tap_count):
    atoms_here, seg_len = others.shape
    block_count = seg_len // block_width
    lag_blocks = tap_count // block_width
    extended = code_ext.reshape(atoms_here, block_count + lag_blocks, block_width)
    others_blocks = others.reshape(atoms_here, block_count, block_width)
    total = jnp.zeros((atoms_here, tap_count), jnp.float32)
    for offset in range(lag_blocks + 1):
        window = extended[:, lag_blocks - offset : lag_blocks - offset + block_count]
        grad = jnp.einsum(
            "kbm,kbi->kmi", window, others_blocks, preferred_element_type=jnp.float32, precision=highest
        ).reshape(atoms_here, block_width * block_width)
        total = total + jnp.dot(grad, band_sums_matrix(block_width, tap_count, offset), precision=highest)
    return total


def convolve_blocks(matrices, code_rows, before, block_width):
    atoms_here, seg_len = code_rows.shape
    block_count = seg_len // block_width
    lag_blocks = len(matrices) - 1
    extended = jnp.concatenate([before, code_rows], axis=1).reshape(
        atoms_here, block_count + lag_blocks, block_width
    )
    summed = jnp.zeros((atoms_here, block_count, block_width), jnp.float32)
    for offset, matrix in enumerate(matrices):
        window = extended[:, lag_blocks - offset : lag_blocks - offset + block_count]
        summed = summed + jnp.einsum(
            "kbm,kmi->kbi", window, matrix, preferred_element_type=jnp.float32, precision=highest
        )
    return summed.reshape(atoms_here, seg_len)


def correlate_blocks(matrices, residual_b, after_rim, block_width):
    atoms_here, seg_len = residual_b.shape
    block_count = seg_len // block_width
    extended = jnp.concatenate([residual_b, after_rim], axis=1).reshape(
        atoms_here, block_count + len(matrices) - 1, block_width
    )
    summed = jnp.zeros((atoms_here, block_count, block_width), jnp.float32)
    for offset, matrix in enumerate(matrices):
        window = extended[:, offset : offset + block_count]
        summed = summed + jnp.einsum(
            "kbi,kim->kbm", window, matrix, preferred_element_type=jnp.float32, precision=highest
        )
    return summed.reshape(atoms_here, seg_len)


def reconstruct(matrices, latent_rows, block_width, tap_count):
    latent_b = latent_rows.astype(jnp.bfloat16)
    before = passed_along(latent_b[:, latent_b.shape[1] - tap_count :], "seg", 1)
    return (convolve_blocks(matrices, latent_b, before, block_width), before, latent_b)


def on_device(signal, spatial, temporal, start_codes, thresholds, step_sizes, breaks):
    chan_rows, seg_len = signal.shape
    atoms_all, tap_count = temporal.shape
    block_width = 128
    skew = one_hot_skew(block_width, 2 * block_width)
    skew_flipped = one_hot_skew(block_width, 2 * block_width, transposed=True)
    ghost = GHOST_BLOCKS * block_width
    wide_positions = lax.axis_index("seg") * seg_len - ghost + lax.iota(jnp.int32, seg_len + 2 * ghost)
    wide_crosses = (wide_positions[None, :] < breaks[:, None]) & (
        breaks[:, None] < wide_positions[None, :] + tap_count
    )
    inside = jnp.where(
        (wide_positions >= 0) & (wide_positions < seg_len * lax.axis_size("seg")), 1.0, 0.0
    ).astype(jnp.float32)
    allowed_wide = inside * jnp.where(jnp.any(wide_crosses, axis=0), 0.0, 1.0).astype(jnp.float32)
    zero_rim = jnp.zeros((atoms_all, tap_count), jnp.bfloat16)
    raw_start = butterfly_sum(jnp.dot(spatial.T, spatial, precision=highest), "chan")
    scaling = 1.0 / jnp.sqrt(jnp.diag(raw_start) + epsilon)
    space_loc = spatial * scaling[None, :]
    gram_matrix = raw_start * scaling[:, None] * scaling[None, :]
    kernel = temporal / jnp.sqrt(jnp.sum(temporal * temporal, axis=1, keepdims=True) + epsilon)
    latent = start_codes
    for sweep_index in range(OUTER):
        space_b = space_loc.astype(jnp.bfloat16)
        kernel_b = kernel.astype(jnp.bfloat16)
        projected = butterfly_sum(
            jnp.dot(space_b.T, signal, preferred_element_type=jnp.float32), "chan"
        )
        own_gram = gram_matrix

        def mix_atoms(rebuilt_part):
            return jnp.dot(own_gram, rebuilt_part, precision=highest)

        matrices = toeplitz(kernel_b, block_width, skew)
        flipped = toeplitz(kernel_b, block_width, skew_flipped)
        step_col = step_sizes[:, None]
        limit_col = (step_sizes * thresholds)[:, None]

        projected_wide = widened(projected, ghost)

        def stepper(projected_w, inside_w, allowed_w):
            def shrink_step(iteration, carried):
                current, current_b = carried
                rebuilt = convolve_blocks(matrices, current_b, zero_rim, block_width)
                residual = (projected_w - mix_atoms(rebuilt)) * inside_w[None, :]
                descent = correlate_blocks(flipped, residual.astype(jnp.bfloat16), zero_rim, block_width)
                stepped = current + step_col * descent
                shrunk = (
                    allowed_w[None, :]
                    * jnp.sign(stepped)
                    * jnp.maximum(jnp.abs(stepped) - limit_col, 0.0)
                )
                return (shrunk, shrunk.astype(jnp.bfloat16))

            return shrink_step

        narrow = NARROW_BLOCKS * block_width
        cut = ghost - narrow
        narrow_len = seg_len + 2 * narrow
        wide_step = stepper(projected_wide, inside, allowed_wide)
        narrow_step = stepper(
            projected_wide[:, cut : cut + narrow_len], inside[cut : cut + narrow_len], allowed_wide[cut : cut + narrow_len]
        )
        for chunk in range(ITERS // CHUNK):
            wide = widened(latent, ghost)
            wide, wide_b = lax.fori_loop(0, WIDE_STEPS, wide_step, (wide, wide.astype(jnp.bfloat16)))
            carried = (wide[:, cut : cut + narrow_len], wide_b[:, cut : cut + narrow_len])
            wide, _ = lax.fori_loop(0, CHUNK - WIDE_STEPS, narrow_step, carried)
            latent = wide[:, narrow : narrow + seg_len]
        rebuilt, before, latent_b = reconstruct(matrices, latent, block_width, tap_count)
        rebuilt_b = rebuilt.astype(jnp.bfloat16)
        row_part = jnp.dot(rebuilt_b, signal.T, preferred_element_type=jnp.float32)
        others = projected - jnp.dot(
            gram_matrix - jnp.diag(jnp.diag(gram_matrix)), rebuilt, precision=highest
        )
        code_ext = jnp.concatenate([before, latent_b], axis=1)
        taps_part = lag_sums(code_ext, others, block_width, tap_count)
        cross_part = jnp.dot(rebuilt, rebuilt.T, precision=highest)
        joined = butterfly_sum(jnp.concatenate([row_part, cross_part, taps_part], axis=1), "seg")
        stats_rows = joined[:, :chan_rows].T
        cross_gram = joined[:, chan_rows : chan_rows + atoms_all]
        raw_kernel = joined[:, chan_rows + atoms_all :]
        raw_rows = stats_rows - jnp.dot(
            space_loc, cross_gram - jnp.diag(jnp.diag(cross_gram)), precision=highest
        )
        raw_gram = butterfly_sum(jnp.dot(raw_rows.T, raw_rows, precision=highest), "chan")
        scaling = 1.0 / jnp.sqrt(jnp.diag(raw_gram) + epsilon)
        space_loc = raw_rows * scaling[None, :]
        gram_matrix = raw_gram * scaling[:, None] * scaling[None, :]
        kernel = raw_kernel / jnp.sqrt(
            jnp.sum(raw_kernel * raw_kernel, axis=1, keepdims=True) + epsilon
        )
    return (latent, space_loc, kernel)


def solution(mesh):
    placed = (P("chan", "seg"), P("chan", None), P(), P(None, "seg"), P(), P(), P())
    return jax.shard_map(
        on_device,
        mesh=mesh,
        in_specs=placed,
        out_specs=(P(None, "seg"), P("chan", None), P()),
        check_vma=False,
    )
```

```python
import jax
import jax.numpy as jnp
from jax import lax
from jax.sharding import PartitionSpec as P

ITERS = 10
OUTER = 2
CHUNK = 5
GHOST_BLOCKS = 10


epsilon = 1e-06
highest = lax.Precision.HIGHEST


def passed_along(value, axis, steps):
    count = lax.axis_size(axis)
    leading, last = (max(0, -steps), min(count, count - steps))
    return lax.ppermute(value, axis, [(source, source + steps) for source in range(leading, last)])


def widened(rows, ghost):
    seg_len = rows.shape[1]
    from_left = passed_along(rows[:, seg_len - ghost :], "seg", 1)
    from_right = passed_along(rows[:, :ghost], "seg", -1)
    return jnp.concatenate([from_left, rows, from_right], axis=1)


def butterfly_sum(value, axis):
    count = lax.axis_size(axis)
    distance = 1
    while distance < count:
        partner = lax.ppermute(value, axis, [(i, i ^ distance) for i in range(count)])
        value = value + partner
        distance *= 2
    return value


def one_hot_skew(block_width, tap_span, transposed=False):
    shape = (tap_span, block_width, block_width)
    d = lax.broadcasted_iota(jnp.int32, shape, 0)
    m = lax.broadcasted_iota(jnp.int32, shape, 2 if transposed else 1)
    i = lax.broadcasted_iota(jnp.int32, shape, 1 if transposed else 2)
    hit = d == i - m + (block_width - 1)
    return jnp.where(hit, 1.0, 0.0).astype(jnp.bfloat16).reshape(tap_span, block_width * block_width)


def band_sums_matrix(block_width, tap_count, offset):
    shape = (block_width, block_width, tap_count)
    m = lax.broadcasted_iota(jnp.int32, shape, 0)
    i = lax.broadcasted_iota(jnp.int32, shape, 1)
    tau = lax.broadcasted_iota(jnp.int32, shape, 2)
    hit = tau == i - m + block_width * offset
    return jnp.where(hit, 1.0, 0.0).reshape(block_width * block_width, tap_count)


def toeplitz(kernel_taps, block_width, skew):
    atoms_here, tap_count = kernel_taps.shape
    zero_pad = jnp.zeros((atoms_here, block_width), kernel_taps.dtype)
    padded = jnp.concatenate([zero_pad, kernel_taps, zero_pad, zero_pad], axis=1)
    lag_blocks = tap_count // block_width
    tap_span = 2 * block_width
    bands = jnp.concatenate(
        [padded[:, off * block_width + 1 : off * block_width + 1 + tap_span] for off in range(lag_blocks + 1)],
        axis=0,
    )
    flat = jnp.dot(bands, skew, preferred_element_type=jnp.float32).astype(kernel_taps.dtype)
    flat = flat.reshape(lag_blocks + 1, atoms_here, block_width, block_width)
    return [flat[off] for off in range(lag_blocks + 1)]


def lag_sums(code_ext, others, block_width, tap_count):
    atoms_here, seg_len = others.shape
    block_count = seg_len // block_width
    lag_blocks = tap_count // block_width
    extended = code_ext.reshape(atoms_here, block_count + lag_blocks, block_width)
    others_blocks = others.reshape(atoms_here, block_count, block_width)
    total = jnp.zeros((atoms_here, tap_count), jnp.float32)
    for offset in range(lag_blocks + 1):
        window = extended[:, lag_blocks - offset : lag_blocks - offset + block_count]
        grad = jnp.einsum(
            "kbm,kbi->kmi", window, others_blocks, preferred_element_type=jnp.float32, precision=highest
        ).reshape(atoms_here, block_width * block_width)
        total = total + jnp.dot(grad, band_sums_matrix(block_width, tap_count, offset), precision=highest)
    return total


def convolve_blocks(matrices, code_rows, before, block_width):
    atoms_here, seg_len = code_rows.shape
    block_count = seg_len // block_width
    lag_blocks = len(matrices) - 1
    extended = jnp.concatenate([before, code_rows], axis=1).reshape(
        atoms_here, block_count + lag_blocks, block_width
    )
    summed = jnp.zeros((atoms_here, block_count, block_width), jnp.float32)
    for offset, matrix in enumerate(matrices):
        window = extended[:, lag_blocks - offset : lag_blocks - offset + block_count]
        summed = summed + jnp.einsum(
            "kbm,kmi->kbi", window, matrix, preferred_element_type=jnp.float32, precision=highest
        )
    return summed.reshape(atoms_here, seg_len)


def correlate_blocks(matrices, residual_b, after_rim, block_width):
    atoms_here, seg_len = residual_b.shape
    block_count = seg_len // block_width
    extended = jnp.concatenate([residual_b, after_rim], axis=1).reshape(
        atoms_here, block_count + len(matrices) - 1, block_width
    )
    summed = jnp.zeros((atoms_here, block_count, block_width), jnp.float32)
    for offset, matrix in enumerate(matrices):
        window = extended[:, offset : offset + block_count]
        summed = summed + jnp.einsum(
            "kbi,kim->kbm", window, matrix, preferred_element_type=jnp.float32, precision=highest
        )
    return summed.reshape(atoms_here, seg_len)


def reconstruct(matrices, latent_rows, block_width, tap_count):
    latent_b = latent_rows.astype(jnp.bfloat16)
    before = passed_along(latent_b[:, latent_b.shape[1] - tap_count :], "seg", 1)
    return (convolve_blocks(matrices, latent_b, before, block_width), before, latent_b)


def on_device(signal, spatial, temporal, start_codes, thresholds, step_sizes, breaks):
    chan_rows, seg_len = signal.shape
    atoms_all, tap_count = temporal.shape
    block_width = 128
    skew = one_hot_skew(block_width, 2 * block_width)
    skew_flipped = one_hot_skew(block_width, 2 * block_width, transposed=True)
    ghost = GHOST_BLOCKS * block_width
    wide_positions = lax.axis_index("seg") * seg_len - ghost + lax.iota(jnp.int32, seg_len + 2 * ghost)
    wide_crosses = (wide_positions[None, :] < breaks[:, None]) & (
        breaks[:, None] < wide_positions[None, :] + tap_count
    )
    inside = jnp.where(
        (wide_positions >= 0) & (wide_positions < seg_len * lax.axis_size("seg")), 1.0, 0.0
    ).astype(jnp.float32)
    allowed_wide = inside * jnp.where(jnp.any(wide_crosses, axis=0), 0.0, 1.0).astype(jnp.float32)
    zero_rim = jnp.zeros((atoms_all, tap_count), jnp.bfloat16)
    raw_start = butterfly_sum(jnp.dot(spatial.T, spatial, precision=highest), "chan")
    scaling = 1.0 / jnp.sqrt(jnp.diag(raw_start) + epsilon)
    space_loc = spatial * scaling[None, :]
    gram_matrix = raw_start * scaling[:, None] * scaling[None, :]
    kernel = temporal / jnp.sqrt(jnp.sum(temporal * temporal, axis=1, keepdims=True) + epsilon)
    latent = start_codes
    for sweep_index in range(OUTER):
        space_b = space_loc.astype(jnp.bfloat16)
        kernel_b = kernel.astype(jnp.bfloat16)
        projected = butterfly_sum(
            jnp.dot(space_b.T, signal, preferred_element_type=jnp.float32), "chan"
        )
        own_gram = gram_matrix

        def mix_atoms(rebuilt_part):
            return jnp.dot(own_gram, rebuilt_part, precision=highest)

        matrices = toeplitz(kernel_b, block_width, skew)
        flipped = toeplitz(kernel_b, block_width, skew_flipped)
        step_col = step_sizes[:, None]
        limit_col = (step_sizes * thresholds)[:, None]

        both_wide = widened(jnp.concatenate([projected, latent], axis=0), ghost)
        projected_wide = both_wide[:atoms_all]

        def shrink_step(iteration, carried):
            current, current_b = carried
            rebuilt = convolve_blocks(matrices, current_b, zero_rim, block_width)
            residual = (projected_wide - mix_atoms(rebuilt)) * inside[None, :]
            descent = correlate_blocks(flipped, residual.astype(jnp.bfloat16), zero_rim, block_width)
            stepped = current + step_col * descent
            shrunk = (
                allowed_wide[None, :]
                * jnp.sign(stepped)
                * jnp.maximum(jnp.abs(stepped) - limit_col, 0.0)
            )
            return (shrunk, shrunk.astype(jnp.bfloat16))

        for chunk in range(ITERS // CHUNK):
            wide = both_wide[atoms_all:] if chunk == 0 else widened(latent, ghost)
            wide, _ = lax.fori_loop(0, CHUNK, shrink_step, (wide, wide.astype(jnp.bfloat16)))
            latent = wide[:, ghost : ghost + seg_len]
        rebuilt, before, latent_b = reconstruct(matrices, latent, block_width, tap_count)
        rebuilt_b = rebuilt.astype(jnp.bfloat16)
        row_part = jnp.dot(rebuilt_b, signal.T, preferred_element_type=jnp.float32)
        others = projected - jnp.dot(
            gram_matrix - jnp.diag(jnp.diag(gram_matrix)), rebuilt, precision=highest
        )
        code_ext = jnp.concatenate([before, latent_b], axis=1)
        taps_part = lag_sums(code_ext, others, block_width, tap_count)
        cross_part = jnp.dot(rebuilt, rebuilt.T, precision=highest)
        joined = butterfly_sum(jnp.concatenate([row_part, cross_part, taps_part], axis=1), "seg")
        stats_rows = joined[:, :chan_rows].T
        cross_gram = joined[:, chan_rows : chan_rows + atoms_all]
        raw_kernel = joined[:, chan_rows + atoms_all :]
        raw_rows = stats_rows - jnp.dot(
            space_loc, cross_gram - jnp.diag(jnp.diag(cross_gram)), precision=highest
        )
        raw_gram = butterfly_sum(jnp.dot(raw_rows.T, raw_rows, precision=highest), "chan")
        scaling = 1.0 / jnp.sqrt(jnp.diag(raw_gram) + epsilon)
        space_loc = raw_rows * scaling[None, :]
        gram_matrix = raw_gram * scaling[:, None] * scaling[None, :]
        kernel = raw_kernel / jnp.sqrt(
            jnp.sum(raw_kernel * raw_kernel, axis=1, keepdims=True) + epsilon
        )
    return (latent, space_loc, kernel)


def solution(mesh):
    placed = (P("chan", "seg"), P("chan", None), P(), P(None, "seg"), P(), P(), P())
    return jax.shard_map(
        on_device,
        mesh=mesh,
        in_specs=placed,
        out_specs=(P(None, "seg"), P("chan", None), P()),
        check_vma=False,
    )
```

```python
import jax
import jax.numpy as jnp
from jax import lax
from jax.sharding import PartitionSpec as P

ITERS = 10
OUTER = 2
CHUNK = 5
GHOST_BLOCKS = 12


epsilon = 1e-06
highest = lax.Precision.HIGHEST


def passed_along(value, axis, steps):
    count = lax.axis_size(axis)
    leading, last = (max(0, -steps), min(count, count - steps))
    return lax.ppermute(value, axis, [(source, source + steps) for source in range(leading, last)])


def widened(rows, ghost):
    seg_len = rows.shape[1]
    from_left = passed_along(rows[:, seg_len - ghost :], "seg", 1)
    from_right = passed_along(rows[:, :ghost], "seg", -1)
    return jnp.concatenate([from_left, rows, from_right], axis=1)


def butterfly_sum(value, axis):
    count = lax.axis_size(axis)
    distance = 1
    while distance < count:
        partner = lax.ppermute(value, axis, [(i, i ^ distance) for i in range(count)])
        value = value + partner
        distance *= 2
    return value


def one_hot_skew(block_width, tap_span, transposed=False):
    shape = (tap_span, block_width, block_width)
    d = lax.broadcasted_iota(jnp.int32, shape, 0)
    m = lax.broadcasted_iota(jnp.int32, shape, 2 if transposed else 1)
    i = lax.broadcasted_iota(jnp.int32, shape, 1 if transposed else 2)
    hit = d == i - m + (block_width - 1)
    return jnp.where(hit, 1.0, 0.0).astype(jnp.bfloat16).reshape(tap_span, block_width * block_width)


def band_sums_matrix(block_width, tap_count, offset):
    shape = (block_width, block_width, tap_count)
    m = lax.broadcasted_iota(jnp.int32, shape, 0)
    i = lax.broadcasted_iota(jnp.int32, shape, 1)
    tau = lax.broadcasted_iota(jnp.int32, shape, 2)
    hit = tau == i - m + block_width * offset
    return jnp.where(hit, 1.0, 0.0).reshape(block_width * block_width, tap_count)


def toeplitz(kernel_taps, block_width, skew):
    atoms_here, tap_count = kernel_taps.shape
    zero_pad = jnp.zeros((atoms_here, block_width), kernel_taps.dtype)
    padded = jnp.concatenate([zero_pad, kernel_taps, zero_pad, zero_pad], axis=1)
    lag_blocks = tap_count // block_width
    tap_span = 2 * block_width
    bands = jnp.concatenate(
        [padded[:, off * block_width + 1 : off * block_width + 1 + tap_span] for off in range(lag_blocks + 1)],
        axis=0,
    )
    flat = jnp.dot(bands, skew, preferred_element_type=jnp.float32).astype(kernel_taps.dtype)
    flat = flat.reshape(lag_blocks + 1, atoms_here, block_width, block_width)
    return [flat[off] for off in range(lag_blocks + 1)]


def lag_sums(code_ext, others, block_width, tap_count):
    atoms_here, seg_len = others.shape
    block_count = seg_len // block_width
    lag_blocks = tap_count // block_width
    extended = code_ext.reshape(atoms_here, block_count + lag_blocks, block_width)
    others_blocks = others.reshape(atoms_here, block_count, block_width)
    total = jnp.zeros((atoms_here, tap_count), jnp.float32)
    for offset in range(lag_blocks + 1):
        window = extended[:, lag_blocks - offset : lag_blocks - offset + block_count]
        grad = jnp.einsum(
            "kbm,kbi->kmi", window, others_blocks, preferred_element_type=jnp.float32, precision=highest
        ).reshape(atoms_here, block_width * block_width)
        total = total + jnp.dot(grad, band_sums_matrix(block_width, tap_count, offset), precision=highest)
    return total


def convolve_blocks(matrices, code_rows, before, block_width):
    atoms_here, seg_len = code_rows.shape
    block_count = seg_len // block_width
    lag_blocks = len(matrices) - 1
    extended = jnp.concatenate([before, code_rows], axis=1).reshape(
        atoms_here, block_count + lag_blocks, block_width
    )
    summed = jnp.zeros((atoms_here, block_count, block_width), jnp.float32)
    for offset, matrix in enumerate(matrices):
        window = extended[:, lag_blocks - offset : lag_blocks - offset + block_count]
        summed = summed + jnp.einsum(
            "kbm,kmi->kbi", window, matrix, preferred_element_type=jnp.float32, precision=highest
        )
    return summed.reshape(atoms_here, seg_len)


def correlate_blocks(matrices, residual_b, after_rim, block_width):
    atoms_here, seg_len = residual_b.shape
    block_count = seg_len // block_width
    extended = jnp.concatenate([residual_b, after_rim], axis=1).reshape(
        atoms_here, block_count + len(matrices) - 1, block_width
    )
    summed = jnp.zeros((atoms_here, block_count, block_width), jnp.float32)
    for offset, matrix in enumerate(matrices):
        window = extended[:, offset : offset + block_count]
        summed = summed + jnp.einsum(
            "kbi,kim->kbm", window, matrix, preferred_element_type=jnp.float32, precision=highest
        )
    return summed.reshape(atoms_here, seg_len)


def reconstruct(matrices, latent_rows, block_width, tap_count):
    latent_b = latent_rows.astype(jnp.bfloat16)
    before = passed_along(latent_b[:, latent_b.shape[1] - tap_count :], "seg", 1)
    return (convolve_blocks(matrices, latent_b, before, block_width), before, latent_b)


def on_device(signal, spatial, temporal, start_codes, thresholds, step_sizes, breaks):
    chan_rows, seg_len = signal.shape
    atoms_all, tap_count = temporal.shape
    block_width = 128
    skew = one_hot_skew(block_width, 2 * block_width)
    skew_flipped = one_hot_skew(block_width, 2 * block_width, transposed=True)
    ghost = GHOST_BLOCKS * block_width
    wide_positions = lax.axis_index("seg") * seg_len - ghost + lax.iota(jnp.int32, seg_len + 2 * ghost)
    wide_crosses = (wide_positions[None, :] < breaks[:, None]) & (
        breaks[:, None] < wide_positions[None, :] + tap_count
    )
    inside = jnp.where(
        (wide_positions >= 0) & (wide_positions < seg_len * lax.axis_size("seg")), 1.0, 0.0
    ).astype(jnp.float32)
    allowed_wide = inside * jnp.where(jnp.any(wide_crosses, axis=0), 0.0, 1.0).astype(jnp.float32)
    zero_rim = jnp.zeros((atoms_all, tap_count), jnp.bfloat16)
    raw_start = butterfly_sum(jnp.dot(spatial.T, spatial, precision=highest), "chan")
    scaling = 1.0 / jnp.sqrt(jnp.diag(raw_start) + epsilon)
    space_loc = spatial * scaling[None, :]
    gram_matrix = raw_start * scaling[:, None] * scaling[None, :]
    kernel = temporal / jnp.sqrt(jnp.sum(temporal * temporal, axis=1, keepdims=True) + epsilon)
    latent = start_codes
    for sweep_index in range(OUTER):
        space_b = space_loc.astype(jnp.bfloat16)
        kernel_b = kernel.astype(jnp.bfloat16)
        projected = butterfly_sum(
            jnp.dot(space_b.T, signal, preferred_element_type=jnp.float32), "chan"
        )
        own_gram = gram_matrix

        def mix_atoms(rebuilt_part):
            return jnp.dot(own_gram, rebuilt_part, precision=highest)

        matrices = toeplitz(kernel_b, block_width, skew)
        flipped = toeplitz(kernel_b, block_width, skew_flipped)
        step_col = step_sizes[:, None]
        limit_col = (step_sizes * thresholds)[:, None]

        both_wide = widened(jnp.concatenate([projected, latent], axis=0), ghost)
        projected_wide = both_wide[:atoms_all]

        def shrink_step(iteration, carried):
            current, current_b = carried
            rebuilt = convolve_blocks(matrices, current_b, zero_rim, block_width)
            residual = (projected_wide - mix_atoms(rebuilt)) * inside[None, :]
            descent = correlate_blocks(flipped, residual.astype(jnp.bfloat16), zero_rim, block_width)
            stepped = current + step_col * descent
            shrunk = (
                allowed_wide[None, :]
                * jnp.sign(stepped)
                * jnp.maximum(jnp.abs(stepped) - limit_col, 0.0)
            )
            return (shrunk, shrunk.astype(jnp.bfloat16))

        for chunk in range(ITERS // CHUNK):
            wide = both_wide[atoms_all:] if chunk == 0 else widened(latent, ghost)
            wide, _ = lax.fori_loop(0, CHUNK, shrink_step, (wide, wide.astype(jnp.bfloat16)))
            latent = wide[:, ghost : ghost + seg_len]
        before = wide[:, ghost - tap_count : ghost].astype(jnp.bfloat16)
        latent_b = latent.astype(jnp.bfloat16)
        rebuilt = convolve_blocks(matrices, latent_b, before, block_width)
        rebuilt_b = rebuilt.astype(jnp.bfloat16)
        row_part = jnp.dot(rebuilt_b, signal.T, preferred_element_type=jnp.float32)
        others = projected - jnp.dot(
            gram_matrix - jnp.diag(jnp.diag(gram_matrix)), rebuilt, precision=highest
        )
        code_ext = jnp.concatenate([before, latent_b], axis=1)
        taps_part = lag_sums(code_ext, others, block_width, tap_count)
        cross_part = jnp.dot(rebuilt, rebuilt.T, precision=highest)
        joined = butterfly_sum(jnp.concatenate([row_part, cross_part, taps_part], axis=1), "seg")
        stats_rows = joined[:, :chan_rows].T
        cross_gram = joined[:, chan_rows : chan_rows + atoms_all]
        raw_kernel = joined[:, chan_rows + atoms_all :]
        raw_rows = stats_rows - jnp.dot(
            space_loc, cross_gram - jnp.diag(jnp.diag(cross_gram)), precision=highest
        )
        raw_gram = butterfly_sum(jnp.dot(raw_rows.T, raw_rows, precision=highest), "chan")
        scaling = 1.0 / jnp.sqrt(jnp.diag(raw_gram) + epsilon)
        space_loc = raw_rows * scaling[None, :]
        gram_matrix = raw_gram * scaling[:, None] * scaling[None, :]
        kernel = raw_kernel / jnp.sqrt(
            jnp.sum(raw_kernel * raw_kernel, axis=1, keepdims=True) + epsilon
        )
    return (latent, space_loc, kernel)


def solution(mesh):
    placed = (P("chan", "seg"), P("chan", None), P(), P(None, "seg"), P(), P(), P())
    return jax.shard_map(
        on_device,
        mesh=mesh,
        in_specs=placed,
        out_specs=(P(None, "seg"), P("chan", None), P()),
        check_vma=False,
    )
```

```python
import jax
import jax.numpy as jnp
from jax import lax
from jax.sharding import PartitionSpec as P

ITERS = 10
OUTER = 2
CHUNK = 5
GHOST_BLOCKS = 10


epsilon = 1e-06
highest = lax.Precision.HIGHEST


def passed_along(value, axis, steps):
    count = lax.axis_size(axis)
    leading, last = (max(0, -steps), min(count, count - steps))
    return lax.ppermute(value, axis, [(source, source + steps) for source in range(leading, last)])


def widened(rows, ghost):
    seg_len = rows.shape[1]
    from_left = passed_along(rows[:, seg_len - ghost :], "seg", 1)
    from_right = passed_along(rows[:, :ghost], "seg", -1)
    return jnp.concatenate([from_left, rows, from_right], axis=1)


def butterfly_sum(value, axis):
    count = lax.axis_size(axis)
    distance = 1
    while distance < count:
        partner = lax.ppermute(value, axis, [(i, i ^ distance) for i in range(count)])
        value = value + partner
        distance *= 2
    return value


def dense_sum(square, axis):
    rows, cols = square.shape
    return butterfly_sum(square.reshape(rows * cols // 128, 128), axis).reshape(rows, cols)


def one_hot_skew(block_width, tap_span, transposed=False):
    shape = (tap_span, block_width, block_width)
    d = lax.broadcasted_iota(jnp.int32, shape, 0)
    m = lax.broadcasted_iota(jnp.int32, shape, 2 if transposed else 1)
    i = lax.broadcasted_iota(jnp.int32, shape, 1 if transposed else 2)
    hit = d == i - m + (block_width - 1)
    return jnp.where(hit, 1.0, 0.0).astype(jnp.bfloat16).reshape(tap_span, block_width * block_width)


def band_sums_matrix(block_width, tap_count, offset):
    shape = (block_width, block_width, tap_count)
    m = lax.broadcasted_iota(jnp.int32, shape, 0)
    i = lax.broadcasted_iota(jnp.int32, shape, 1)
    tau = lax.broadcasted_iota(jnp.int32, shape, 2)
    hit = tau == i - m + block_width * offset
    return jnp.where(hit, 1.0, 0.0).reshape(block_width * block_width, tap_count)


def toeplitz(kernel_taps, block_width, skew):
    atoms_here, tap_count = kernel_taps.shape
    zero_pad = jnp.zeros((atoms_here, block_width), kernel_taps.dtype)
    padded = jnp.concatenate([zero_pad, kernel_taps, zero_pad, zero_pad], axis=1)
    lag_blocks = tap_count // block_width
    tap_span = 2 * block_width
    bands = jnp.concatenate(
        [padded[:, off * block_width + 1 : off * block_width + 1 + tap_span] for off in range(lag_blocks + 1)],
        axis=0,
    )
    flat = jnp.dot(bands, skew, preferred_element_type=jnp.float32).astype(kernel_taps.dtype)
    flat = flat.reshape(lag_blocks + 1, atoms_here, block_width, block_width)
    return [flat[off] for off in range(lag_blocks + 1)]


def lag_sums(code_ext, others, block_width, tap_count):
    atoms_here, seg_len = others.shape
    block_count = seg_len // block_width
    lag_blocks = tap_count // block_width
    extended = code_ext.reshape(atoms_here, block_count + lag_blocks, block_width)
    others_blocks = others.reshape(atoms_here, block_count, block_width)
    total = jnp.zeros((atoms_here, tap_count), jnp.float32)
    for offset in range(lag_blocks + 1):
        window = extended[:, lag_blocks - offset : lag_blocks - offset + block_count]
        grad = jnp.einsum(
            "kbm,kbi->kmi", window, others_blocks, preferred_element_type=jnp.float32, precision=highest
        ).reshape(atoms_here, block_width * block_width)
        total = total + jnp.dot(grad, band_sums_matrix(block_width, tap_count, offset), precision=highest)
    return total


def convolve_blocks(matrices, code_rows, before, block_width):
    atoms_here, seg_len = code_rows.shape
    block_count = seg_len // block_width
    lag_blocks = len(matrices) - 1
    extended = jnp.concatenate([before, code_rows], axis=1).reshape(
        atoms_here, block_count + lag_blocks, block_width
    )
    summed = jnp.zeros((atoms_here, block_count, block_width), jnp.float32)
    for offset, matrix in enumerate(matrices):
        window = extended[:, lag_blocks - offset : lag_blocks - offset + block_count]
        summed = summed + jnp.einsum(
            "kbm,kmi->kbi", window, matrix, preferred_element_type=jnp.float32, precision=highest
        )
    return summed.reshape(atoms_here, seg_len)


def correlate_blocks(matrices, residual_b, after_rim, block_width):
    atoms_here, seg_len = residual_b.shape
    block_count = seg_len // block_width
    extended = jnp.concatenate([residual_b, after_rim], axis=1).reshape(
        atoms_here, block_count + len(matrices) - 1, block_width
    )
    summed = jnp.zeros((atoms_here, block_count, block_width), jnp.float32)
    for offset, matrix in enumerate(matrices):
        window = extended[:, offset : offset + block_count]
        summed = summed + jnp.einsum(
            "kbi,kim->kbm", window, matrix, preferred_element_type=jnp.float32, precision=highest
        )
    return summed.reshape(atoms_here, seg_len)


def reconstruct(matrices, latent_rows, block_width, tap_count):
    latent_b = latent_rows.astype(jnp.bfloat16)
    before = passed_along(latent_b[:, latent_b.shape[1] - tap_count :], "seg", 1)
    return (convolve_blocks(matrices, latent_b, before, block_width), before, latent_b)


def on_device(signal, spatial, temporal, start_codes, thresholds, step_sizes, breaks):
    chan_rows, seg_len = signal.shape
    atoms_all, tap_count = temporal.shape
    block_width = 128
    skew = one_hot_skew(block_width, 2 * block_width)
    skew_flipped = one_hot_skew(block_width, 2 * block_width, transposed=True)
    ghost = GHOST_BLOCKS * block_width
    wide_positions = lax.axis_index("seg") * seg_len - ghost + lax.iota(jnp.int32, seg_len + 2 * ghost)
    wide_crosses = (wide_positions[None, :] < breaks[:, None]) & (
        breaks[:, None] < wide_positions[None, :] + tap_count
    )
    inside = jnp.where(
        (wide_positions >= 0) & (wide_positions < seg_len * lax.axis_size("seg")), 1.0, 0.0
    ).astype(jnp.float32)
    allowed_wide = inside * jnp.where(jnp.any(wide_crosses, axis=0), 0.0, 1.0).astype(jnp.float32)
    zero_rim = jnp.zeros((atoms_all, tap_count), jnp.bfloat16)
    raw_start = dense_sum(jnp.dot(spatial.T, spatial, precision=highest), "chan")
    scaling = 1.0 / jnp.sqrt(jnp.diag(raw_start) + epsilon)
    space_loc = spatial * scaling[None, :]
    gram_matrix = raw_start * scaling[:, None] * scaling[None, :]
    kernel = temporal / jnp.sqrt(jnp.sum(temporal * temporal, axis=1, keepdims=True) + epsilon)
    latent = start_codes
    for sweep_index in range(OUTER):
        space_b = space_loc.astype(jnp.bfloat16)
        kernel_b = kernel.astype(jnp.bfloat16)
        projected = butterfly_sum(
            jnp.dot(space_b.T, signal, preferred_element_type=jnp.float32), "chan"
        )
        own_gram = gram_matrix

        def mix_atoms(rebuilt_part):
            return jnp.dot(own_gram, rebuilt_part, precision=highest)

        matrices = toeplitz(kernel_b, block_width, skew)
        flipped = toeplitz(kernel_b, block_width, skew_flipped)
        step_col = step_sizes[:, None]
        limit_col = (step_sizes * thresholds)[:, None]

        both_wide = widened(jnp.concatenate([projected, latent], axis=0), ghost)
        projected_wide = both_wide[:atoms_all]

        def shrink_step(iteration, carried):
            current, current_b = carried
            rebuilt = convolve_blocks(matrices, current_b, zero_rim, block_width)
            residual = (projected_wide - mix_atoms(rebuilt)) * inside[None, :]
            descent = correlate_blocks(flipped, residual.astype(jnp.bfloat16), zero_rim, block_width)
            stepped = current + step_col * descent
            shrunk = (
                allowed_wide[None, :]
                * jnp.sign(stepped)
                * jnp.maximum(jnp.abs(stepped) - limit_col, 0.0)
            )
            return (shrunk, shrunk.astype(jnp.bfloat16))

        for chunk in range(ITERS // CHUNK):
            wide = both_wide[atoms_all:] if chunk == 0 else widened(latent, ghost)
            wide, _ = lax.fori_loop(0, CHUNK, shrink_step, (wide, wide.astype(jnp.bfloat16)))
            latent = wide[:, ghost : ghost + seg_len]
        rebuilt, before, latent_b = reconstruct(matrices, latent, block_width, tap_count)
        rebuilt_b = rebuilt.astype(jnp.bfloat16)
        row_part = jnp.dot(rebuilt_b, signal.T, preferred_element_type=jnp.float32)
        others = projected - jnp.dot(
            gram_matrix - jnp.diag(jnp.diag(gram_matrix)), rebuilt, precision=highest
        )
        code_ext = jnp.concatenate([before, latent_b], axis=1)
        taps_part = lag_sums(code_ext, others, block_width, tap_count)
        cross_part = jnp.dot(rebuilt, rebuilt.T, precision=highest)
        joined = butterfly_sum(jnp.concatenate([row_part, cross_part, taps_part], axis=1), "seg")
        stats_rows = joined[:, :chan_rows].T
        cross_gram = joined[:, chan_rows : chan_rows + atoms_all]
        raw_kernel = joined[:, chan_rows + atoms_all :]
        raw_rows = stats_rows - jnp.dot(
            space_loc, cross_gram - jnp.diag(jnp.diag(cross_gram)), precision=highest
        )
        raw_gram = dense_sum(jnp.dot(raw_rows.T, raw_rows, precision=highest), "chan")
        scaling = 1.0 / jnp.sqrt(jnp.diag(raw_gram) + epsilon)
        space_loc = raw_rows * scaling[None, :]
        gram_matrix = raw_gram * scaling[:, None] * scaling[None, :]
        kernel = raw_kernel / jnp.sqrt(
            jnp.sum(raw_kernel * raw_kernel, axis=1, keepdims=True) + epsilon
        )
    return (latent, space_loc, kernel)


def solution(mesh):
    placed = (P("chan", "seg"), P("chan", None), P(), P(None, "seg"), P(), P(), P())
    return jax.shard_map(
        on_device,
        mesh=mesh,
        in_specs=placed,
        out_specs=(P(None, "seg"), P("chan", None), P()),
        check_vma=False,
    )
```
